512 devices in a mesh: section: 8 (over z_lo, x), fsdp: 64 (over z_hi, y, core).
Axes of the slice: x: 4, y: 8, z: 8 (z_hi: 4, z_lo: 2; z = z_hi * 2 + z_lo), core: 2. Of those that a mesh axis runs over, the one named last changes fastest.
Arguments:
- activations: bfloat16 [10240, 6144], P('fsdp'), may hold values from -36 to 36
- keep: int32 [10240], P('fsdp'), may hold values from 0 to 1, as said below
- gains: bfloat16 [8, 6144], P('section'), may hold values from 0.099609375 to 1.8984375
- up_rows: int32 [8, 192, 2], P('section'), may hold values from 0 to 95
- up_blocks: bfloat16 [8, 384, 4096], P('section', 'fsdp'), may hold values from -0.5 to 0.5
- down_rows: int32 [8, 96, 2], P('section'), may hold values from 0 to 191
- down_blocks: bfloat16 [8, 192, 4096], P('section', 'fsdp'), may hold values from -0.5 to 0.5
Outputs:
- section_out: bfloat16 [8, 10240, 6144], P('section', 'fsdp')
The draws below stay inside these ranges and needn't reach their ends.
Inputs may be any that keep to these rules, and one draw needn't show every extreme that they name: `keep`: each aligned block of 160 tokens (the tokens of one index of fsdp) holds exactly 128 ones.
All inputs are finite; a program needn't handle non-finite values.
Results may differ from the reference program's by a relative error of at most 0.012.
Values may be sent and summed in bfloat16 or wider, within the bound.
No kernel may reach another device: no remote copies, remote signals or barrier semaphores. Data moves between devices by JAX's collectives and lax.ppermute only.
A program may use at most 128 MiB of HBM per device.

```python
import math
import jax
import jax.numpy as jnp
from jax import lax

D = 6144
FF = 12288
BLK = 64
UP_DEPTH = 2
DOWN_DEPTH = 2
KEEP_DEV = 128
TOK_DEV = 160
TOKENS = 10240
LAYERS = 8
N_FSDP = 64


def draw_activations(key, part):
    first, second, third = jax.random.split(key, 3)
    row_scale = 0.3 * jnp.exp(jax.random.uniform(second, (TOKENS, 1), jnp.float32) * math.log(10.0))
    col_scale = 0.3 * jnp.exp(jax.random.uniform(third, (1, D), jnp.float32) * math.log(10.0))
    base = jax.random.truncated_normal(first, -4.0, 4.0, (TOKENS, D), jnp.float32)
    return (base * row_scale * col_scale).astype(jnp.bfloat16)


def draw_keep(key, part):
    groups = TOKENS // TOK_DEV
    keys = jax.random.split(key, groups)
    orders = jax.vmap(lambda single: jax.random.permutation(single, TOK_DEV))(keys)
    return (orders < KEEP_DEV).astype(jnp.int32).reshape(TOKENS)


def butterfly_rows(key, columns, rows, depth):
    ratio = max(rows // columns, 1)
    strides = list(range(min(ratio, depth - 1)))
    reach = ratio
    while len(strides) < depth - 1:
        strides.append(reach)
        reach = reach * 2
    first, second = jax.random.split(key)
    offset = jax.random.randint(first, (LAYERS, 1, 1), 0, rows)
    shared = jax.random.randint(second, (LAYERS, 1, 1), 0, rows)
    base = (jnp.arange(columns, dtype=jnp.int32) * rows // columns)[None, :, None]
    band = (base + offset + jnp.array(strides, jnp.int32)[None, None, :]) % rows
    shared = jnp.broadcast_to(shared, (LAYERS, columns, 1))
    return jnp.concatenate([band, shared], axis=2).astype(jnp.int32)


def draw_up_rows(key, part):
    return butterfly_rows(jax.random.fold_in(key, 11), FF // BLK, D // BLK, UP_DEPTH)


def draw_down_rows(key, part):
    return butterfly_rows(jax.random.fold_in(key, 23), D // BLK, FF // BLK, DOWN_DEPTH)


def block_scale(stream_key, dims, cuts, least, high):
    loudness, own = 1.0, jax.random.fold_in(stream_key, 6)
    for dim, parts in cuts:
        heights = jnp.exp(jax.random.uniform(jax.random.fold_in(own, dim), (parts,), jnp.float32, least / len(cuts), high / len(cuts)))
        loudness = loudness * jnp.repeat(heights, dims[dim] // parts).reshape([-1 if axis == dim else 1 for axis in range(len(dims))])
    return loudness


def scatter_about(own_key, shape, deviation, limit, pieces=(), kind=jnp.bfloat16):
    entries = jax.random.normal(own_key, shape, jnp.float32) * deviation
    if len(pieces) > 0:
        entries = block_scale(own_key, shape, pieces, -0.22, 0.18) * entries
    return jnp.clip(entries, min=-limit, max=limit).astype(kind)


def setup_inputs(seed: int = 0) -> dict:
    splits = jax.random.split(jax.random.key(seed), 8)
    return {
        "activations": draw_activations(jax.random.fold_in(splits[7], 71), 0),
        "keep": draw_keep(jax.random.fold_in(splits[7], 71), 0),
        "gains": jnp.clip(1.0 + 0.18 * jax.random.normal(splits[2], (LAYERS, D), jnp.float32), 0.099609375, 1.8984375).astype(jnp.bfloat16),
        "up_rows": draw_up_rows(jax.random.fold_in(splits[7], 71), 0),
        "up_blocks": scatter_about(splits[4], (LAYERS, (FF // BLK) * UP_DEPTH, BLK * BLK), (UP_DEPTH * BLK) ** -0.5, 0.5, ((0, 8), (1, 64))),
        "down_rows": draw_down_rows(jax.random.fold_in(splits[7], 71), 0),
        "down_blocks": scatter_about(splits[6], (LAYERS, (D // BLK) * DOWN_DEPTH, BLK * BLK), (DOWN_DEPTH * BLK) ** -0.5, 0.5, ((0, 8), (1, 64))),
    }


def apply_layer(carried, gain, up_index, up_values, down_index, down_values):
    count = carried.shape[0]
    blocks_in = D // BLK
    blocks_hid = FF // BLK
    wide = carried.astype(jnp.float32)
    meansq = lax.optimization_barrier(jnp.mean(wide * wide, axis=-1, keepdims=True))
    normed = (wide * lax.rsqrt(meansq + 1e-05) * gain.astype(jnp.float32)).astype(jnp.bfloat16)
    picked = normed.reshape(count, blocks_in, BLK)[:, up_index.reshape(-1).astype(jnp.int32), :]
    picked = picked.reshape(count, blocks_hid, UP_DEPTH * BLK)
    weights_up = up_values.reshape(blocks_hid, UP_DEPTH * BLK, BLK)
    up_sums = jnp.einsum('ncr,crj->ncj', picked.astype(jnp.float32), weights_up.astype(jnp.float32))
    hidden = jax.nn.gelu(up_sums, approximate=True).astype(jnp.bfloat16).reshape(count, FF)
    second = hidden.reshape(count, blocks_hid, BLK)[:, down_index.reshape(-1).astype(jnp.int32), :]
    second = second.reshape(count, blocks_in, DOWN_DEPTH * BLK)
    weights_down = down_values.reshape(blocks_in, DOWN_DEPTH * BLK, BLK)
    down_sums = jnp.einsum('ncr,crj->ncj', second.astype(jnp.float32), weights_down.astype(jnp.float32))
    return down_sums.reshape(count, D)

def reference(activations, keep, gains, up_rows, up_blocks, down_rows, down_blocks):
    kept_total = KEEP_DEV * N_FSDP
    chosen = jnp.nonzero(keep, size=kept_total)[0].astype(jnp.int32)
    carried = activations[chosen]
    results = []
    for layer in range(LAYERS):
        branch = apply_layer(carried, gains[layer], up_rows[layer], up_blocks[layer], down_rows[layer], down_blocks[layer])
        carried = (carried.astype(jnp.float32) + branch).astype(jnp.bfloat16)
        results.append(activations.at[chosen].set(carried))
    return jnp.stack(results)
```

```python
import jax
import jax.numpy as jnp
from jax import lax
from jax.sharding import Mesh
from jax.sharding import PartitionSpec as P

BLK = 64
UP_DEPTH = 2
DOWN_DEPTH = 2
KEEP_DEV = 128

SEC = ("zl", "x")
FS = ("zh", "y", "c")


def from_behind(value, axis, steps):
    count = lax.axis_size(axis)
    initial, last = (max(0, -steps), min(count, count - steps))
    return lax.ppermute(value, axis, [(source, source + steps) for source in range(initial, last)])


def gather_blocks(shard):
    n = shard.shape[1]
    rows = shard.reshape(n * 32, 128)
    rows = lax.all_gather(rows, "zh", axis=0, tiled=True)
    rows = lax.all_gather(rows, ("y", "c"), axis=0, tiled=True)
    zh = lax.axis_size("zh")
    yc = rows.shape[0] // (zh * n * 32)
    rows = rows.reshape(yc, zh, n * 32, 128).transpose(1, 0, 2, 3)
    return rows.reshape(zh * yc * n, 4096)


def make_layer(gain, up_index, up_values, down_index, down_values):
    width = gain.shape[0]
    hidden_width = up_values.shape[0] // UP_DEPTH * BLK
    blocks_in = width // BLK
    blocks_hid = hidden_width // BLK
    weights_up = up_values.reshape(blocks_hid, UP_DEPTH * BLK, BLK)
    weights_down = down_values.reshape(blocks_in, DOWN_DEPTH * BLK, BLK)
    gain_wide = gain.astype(jnp.float32)

    def layer(block):
        count = block.shape[0]
        wide = block.astype(jnp.float32)
        meansq = jnp.mean(wide * wide, axis=-1, keepdims=True)
        normed = (wide * lax.rsqrt(meansq + 1e-05) * gain_wide).astype(jnp.bfloat16)
        picked = normed.reshape(count, blocks_in, BLK)[:, up_index, :]
        picked = picked.reshape(count, blocks_hid, UP_DEPTH * BLK)
        up_sums = jnp.einsum("ncr,crj->ncj", picked, weights_up, preferred_element_type=jnp.float32)
        hidden = jax.nn.gelu(up_sums, approximate=True).astype(jnp.bfloat16)
        second = hidden[:, down_index, :].reshape(count, blocks_in, DOWN_DEPTH * BLK)
        down_sums = jnp.einsum(
            "ncr,crj->ncj", second, weights_down, preferred_element_type=jnp.float32
        )
        return (wide + down_sums.reshape(count, width)).astype(jnp.bfloat16)

    return layer


def per_device(activations, keep, gains, up_rows, up_blocks, down_rows, down_blocks):
    up_all = gather_blocks(up_blocks)
    down_all = gather_blocks(down_blocks)
    apply = make_layer(
        gains[0], up_rows[0].reshape(-1), up_all, down_rows[0].reshape(-1), down_all
    )
    places = jnp.cumsum(keep) - 1
    target = jnp.where(keep == 1, places, KEEP_DEV)
    chosen = (
        jnp.zeros((KEEP_DEV + 1,), jnp.int32)
        .at[target]
        .set(jnp.arange(keep.shape[0], dtype=jnp.int32))[:KEEP_DEV]
    )
    selected = activations[chosen]
    width = selected.shape[1]
    section = lax.axis_index(SEC)
    sections = lax.axis_size(SEC)
    pieces = 8
    group_rows = selected.shape[0] // pieces
    split = selected.reshape(pieces, group_rows, width)

    def advance(turn, held, record):
        offset = turn - section
        entry = jnp.where(section == 0, split[jnp.minimum(turn, pieces - 1)], held)
        active = (offset >= 0) & (offset < pieces)
        result = lax.cond(active, apply, jnp.zeros_like, entry)
        slot = jnp.clip(offset, 0, pieces - 1)
        current = lax.dynamic_index_in_dim(record, slot, 0, keepdims=False)
        updated = jnp.where(active, result, current)
        record = lax.dynamic_update_index_in_dim(record, updated, slot, 0)
        return (result, record)

    def turn_step(turn, carry):
        held, record = carry
        result, record = advance(turn, held, record)
        held = from_behind(result, SEC, 1)
        return (held, record)

    final_turn = sections + pieces - 2
    held, record = lax.fori_loop(0, final_turn, turn_step, (split[0], split))
    result, record = advance(final_turn, held, record)
    final = record.reshape(selected.shape[0], width)
    merged = activations.at[chosen].set(final)
    return merged[None]


def solution(mesh):
    zh = 4
    yc = mesh.shape["fsdp"] // zh
    zl = 2
    xs = mesh.shape["section"] // zl
    devices = mesh.devices.reshape(zl, xs, zh, yc // 2, 2)
    fine = Mesh(devices, ("zl", "x", "zh", "y", "c"))
    return jax.shard_map(
        per_device,
        mesh=fine,
        in_specs=(
            P(FS, None),
            P(FS),
            P(SEC, None),
            P(SEC, None, None),
            P(SEC, FS, None),
            P(SEC, None, None),
            P(SEC, FS, None),
        ),
        out_specs=P(SEC, FS, None),
        check_vma=False,
    )
```

```python
import jax
import jax.numpy as jnp
from jax import lax
from jax.sharding import Mesh
from jax.sharding import PartitionSpec as P

BLK = 64
UP_DEPTH = 2
DOWN_DEPTH = 2
KEEP_DEV = 128

SEC = ("zl", "x")
FS = ("zh", "y", "c")


def from_behind(value, axis, steps):
    count = lax.axis_size(axis)
    initial, last = (max(0, -steps), min(count, count - steps))
    return lax.ppermute(value, axis, [(source, source + steps) for source in range(initial, last)])


def exchange_zh(part):
    count = lax.axis_size("zh")
    own = lax.axis_index("zh")
    got = [part]
    for shift in range(1, count):
        got.append(lax.ppermute(part, "zh", [(i, (i + shift) % count) for i in range(count)]))
    stacked = jnp.stack(got)
    order = (own - jnp.arange(count, dtype=jnp.int32)) % count
    return jnp.take(stacked, order, axis=0)


def gather_up(shard):
    cols = shard.shape[1] // UP_DEPTH
    part = shard.reshape(cols, UP_DEPTH, BLK, BLK).transpose(0, 3, 1, 2)
    part = part.reshape(cols, BLK, UP_DEPTH * BLK)
    full = exchange_zh(part)
    full = lax.all_gather(full, ("y", "c"), axis=1, tiled=True)
    return full.reshape(-1, BLK, UP_DEPTH * BLK)


def gather_rows(shard):
    n = shard.shape[1]
    part = shard.reshape(n * 32, 128)
    full = exchange_zh(part)
    full = lax.all_gather(full, ("y", "c"), axis=1, tiled=True)
    return full.reshape(-1, 4096)


def make_layer(gain, up_index, up_values, down_index, down_values):
    width = gain.shape[0]
    hidden_width = up_values.shape[0] * BLK
    blocks_in = width // BLK
    blocks_hid = hidden_width // BLK
    weights_up = up_values
    weights_down = down_values.reshape(blocks_in, DOWN_DEPTH * BLK, BLK)
    gain_wide = gain.astype(jnp.float32)

    def layer(block):
        count = block.shape[0]
        wide = block.astype(jnp.float32)
        meansq = jnp.mean(wide * wide, axis=-1, keepdims=True)
        normed = (wide * lax.rsqrt(meansq + 1e-05) * gain_wide).astype(jnp.bfloat16)
        picked = normed.reshape(count, blocks_in, BLK)[:, up_index, :]
        picked = picked.reshape(count, blocks_hid, UP_DEPTH * BLK)
        up_sums = jnp.einsum("ncr,cjr->ncj", picked, weights_up, preferred_element_type=jnp.float32)
        hidden = jax.nn.gelu(up_sums, approximate=True).astype(jnp.bfloat16)
        second = hidden[:, down_index, :].reshape(count, blocks_in, DOWN_DEPTH * BLK)
        down_sums = jnp.einsum(
            "ncr,crj->ncj", second, weights_down, preferred_element_type=jnp.float32
        )
        return (wide + down_sums.reshape(count, width)).astype(jnp.bfloat16)

    return layer


def per_device(activations, keep, gains, up_rows, up_blocks, down_rows, down_blocks):
    up_all = gather_up(up_blocks)
    down_all = gather_rows(down_blocks)
    apply = make_layer(
        gains[0], up_rows[0].reshape(-1), up_all, down_rows[0].reshape(-1), down_all
    )
    places = jnp.cumsum(keep) - 1
    target = jnp.where(keep == 1, places, KEEP_DEV)
    chosen = (
        jnp.zeros((KEEP_DEV + 1,), jnp.int32)
        .at[target]
        .set(jnp.arange(keep.shape[0], dtype=jnp.int32))[:KEEP_DEV]
    )
    selected = activations[chosen]
    width = selected.shape[1]
    section = lax.axis_index(SEC)
    sections = lax.axis_size(SEC)
    pieces = 8
    group_rows = selected.shape[0] // pieces
    split = selected.reshape(pieces, group_rows, width)

    def advance(turn, held, record):
        offset = turn - section
        entry = jnp.where(section == 0, split[jnp.minimum(turn, pieces - 1)], held)
        active = (offset >= 0) & (offset < pieces)
        result = lax.cond(active, apply, jnp.zeros_like, entry)
        slot = jnp.clip(offset, 0, pieces - 1)
        current = lax.dynamic_index_in_dim(record, slot, 0, keepdims=False)
        updated = jnp.where(active, result, current)
        record = lax.dynamic_update_index_in_dim(record, updated, slot, 0)
        return (result, record)

    def turn_step(turn, carry):
        held, record = carry
        result, record = advance(turn, held, record)
        held = from_behind(result, SEC, 1)
        return (held, record)

    turns = sections + pieces - 1
    held, record = lax.fori_loop(0, turns, turn_step, (split[0], split))
    final = record.reshape(selected.shape[0], width)
    merged = activations.at[chosen].set(final)
    return merged[None]


def solution(mesh):
    zh = 4
    yc = mesh.shape["fsdp"] // zh
    zl = 2
    xs = mesh.shape["section"] // zl
    devices = mesh.devices.reshape(zl, xs, zh, yc // 2, 2)
    fine = Mesh(devices, ("zl", "x", "zh", "y", "c"))
    return jax.shard_map(
        per_device,
        mesh=fine,
        in_specs=(
            P(FS, None),
            P(FS),
            P(SEC, None),
            P(SEC, None, None),
            P(SEC, FS, None),
            P(SEC, None, None),
            P(SEC, FS, None),
        ),
        out_specs=P(SEC, FS, None),
        check_vma=False,
    )
```

```python
import jax
import jax.numpy as jnp
from jax import lax
from jax.experimental import pallas as pl
from jax.experimental.pallas import tpu as pltpu
from jax.sharding import Mesh
from jax.sharding import PartitionSpec as P

BLK = 64
UP_DEPTH = 2
DOWN_DEPTH = 2
KEEP_DEV = 128

SEC = ("zl", "x")
FS = ("zh", "y", "c")


def from_behind(value, axis, steps):
    count = lax.axis_size(axis)
    initial, last = (max(0, -steps), min(count, count - steps))
    return lax.ppermute(value, axis, [(source, source + steps) for source in range(initial, last)])


def exchange_zh(part):
    count = lax.axis_size("zh")
    own = lax.axis_index("zh")
    got = [part]
    for shift in range(1, count):
        got.append(lax.ppermute(part, "zh", [(i, (i + shift) % count) for i in range(count)]))
    stacked = jnp.stack(got)
    order = (own - jnp.arange(count, dtype=jnp.int32)) % count
    return jnp.take(stacked, order, axis=0)


def gather_up(shard):
    cols = shard.shape[1] // UP_DEPTH
    part = shard.reshape(cols, UP_DEPTH, BLK, BLK).transpose(0, 3, 1, 2)
    part = part.reshape(cols, BLK, UP_DEPTH * BLK)
    full = exchange_zh(part)
    full = lax.all_gather(full, ("y", "c"), axis=1, tiled=True)
    return full.reshape(-1, BLK, UP_DEPTH * BLK)


def gather_rows(shard):
    n = shard.shape[1]
    part = shard.reshape(n * 32, 128)
    full = exchange_zh(part)
    full = lax.all_gather(full, ("y", "c"), axis=1, tiled=True)
    return full.reshape(-1, 4096)


LANE = 128
NT = (((1,), (1,)), ((), ()))


def _gelu(v):
    return 0.5 * v * (1.0 + jnp.tanh(0.7978845608028654 * (v + 0.044715 * (v * v * v))))


def _pick(s_ref, a, b, lane):
    left = s_ref[a % 2, (a + 1) // 2]
    right = s_ref[1 - b % 2, b // 2]
    return jnp.where(lane < BLK, left, right)


def _shifted(prev, cur):
    lane = lax.broadcasted_iota(jnp.int32, cur.shape, 1)
    return jnp.where(lane < BLK, pltpu.roll(prev, BLK, 1), pltpu.roll(cur, BLK, 1))


def _layer_kernel(up_idx, dn_idx, x_ref, g_ref, wu_ref, wd_ref, o_ref, sx_ref, sh_ref):
    count, width = x_ref.shape
    pairs_in = width // LANE
    pairs_hid = wu_ref.shape[0]
    x = x_ref[...].astype(jnp.float32)
    scale = lax.rsqrt(jnp.mean(x * x, axis=1, keepdims=True) + 1e-05)
    zero = jnp.zeros((count, LANE), jnp.bfloat16)
    prev = zero
    for p in range(pairs_in):
        cur = (x[:, p * LANE:(p + 1) * LANE] * scale * g_ref[:, p * LANE:(p + 1) * LANE]).astype(jnp.bfloat16)
        sx_ref[0, p] = cur
        sx_ref[1, p] = _shifted(prev, cur)
        prev = cur
    sx_ref[0, pairs_in] = zero
    sx_ref[1, pairs_in] = _shifted(prev, zero)
    lane = lax.broadcasted_iota(jnp.int32, (count, LANE), 1)

    def up(cp, prev):
        c0 = 2 * cp
        l0 = _pick(sx_ref, up_idx[2 * c0], up_idx[2 * c0 + 1], lane)
        l1 = _pick(sx_ref, up_idx[2 * c0 + 2], up_idx[2 * c0 + 3], lane)
        s = lax.dot_general(l0, wu_ref[cp, 0], NT, preferred_element_type=jnp.float32)
        s = s + lax.dot_general(l1, wu_ref[cp, 1], NT, preferred_element_type=jnp.float32)
        cur = _gelu(s).astype(jnp.bfloat16)
        sh_ref[0, cp] = cur
        sh_ref[1, cp] = _shifted(prev, cur)
        return cur

    last = lax.fori_loop(0, pairs_hid, up, zero, unroll=8)
    sh_ref[0, pairs_hid] = zero
    sh_ref[1, pairs_hid] = _shifted(last, zero)

    for cp in range(pairs_in):
        c0 = 2 * cp
        l0 = _pick(sh_ref, dn_idx[2 * c0], dn_idx[2 * c0 + 1], lane)
        l1 = _pick(sh_ref, dn_idx[2 * c0 + 2], dn_idx[2 * c0 + 3], lane)
        s = lax.dot_general(l0, wd_ref[cp, 0], NT, preferred_element_type=jnp.float32)
        s = s + lax.dot_general(l1, wd_ref[cp, 1], NT, preferred_element_type=jnp.float32)
        o_ref[:, cp * LANE:(cp + 1) * LANE] = (x[:, cp * LANE:(cp + 1) * LANE] + s).astype(jnp.bfloat16)


def pad_pairs(wt):
    cols = wt.shape[0]
    w = wt.reshape(cols // 2, 2, BLK, LANE)
    z = jnp.zeros_like(w[:, :1])
    first = jnp.concatenate([w[:, :1], z], axis=2)
    second = jnp.concatenate([z, w[:, 1:]], axis=2)
    return jnp.concatenate([first, second], axis=1)


def layer(x, gain_row, up_idx, wu_p, dn_idx, wd_p):
    count, width = x.shape
    pairs_in = width // LANE
    pairs_hid = wu_p.shape[0]
    return pl.pallas_call(
        _layer_kernel,
        out_shape=jax.ShapeDtypeStruct((count, width), jnp.bfloat16),
        grid_spec=pltpu.PrefetchScalarGridSpec(
            num_scalar_prefetch=2,
            grid=(1,),
            in_specs=[
                pl.BlockSpec((count, width), lambda i, u, d: (0, 0)),
                pl.BlockSpec((1, width), lambda i, u, d: (0, 0)),
                pl.BlockSpec(wu_p.shape, lambda i, u, d: (0, 0, 0, 0)),
                pl.BlockSpec(wd_p.shape, lambda i, u, d: (0, 0, 0, 0)),
            ],
            out_specs=pl.BlockSpec((count, width), lambda i, u, d: (0, 0)),
            scratch_shapes=[
                pltpu.VMEM((2, pairs_in + 1, count, LANE), jnp.bfloat16),
                pltpu.VMEM((2, pairs_hid + 1, count, LANE), jnp.bfloat16),
            ],
        ),
        compiler_params=pltpu.CompilerParams(vmem_limit_bytes=40 * 1024 * 1024),
    )(up_idx, dn_idx, x, gain_row, wu_p, wd_p)


def column_major_down(rows):
    cols = rows.shape[0] // DOWN_DEPTH
    w = rows.reshape(cols, DOWN_DEPTH, BLK, BLK).transpose(0, 3, 1, 2)
    return w.reshape(cols, BLK, DOWN_DEPTH * BLK)


def make_layer(gain, up_index, up_cols, down_index, down_cols):
    gain_row = gain.astype(jnp.float32)[None, :]
    up_pairs = pad_pairs(up_cols)
    down_pairs = pad_pairs(down_cols)

    def apply(block):
        return layer(block, gain_row, up_index, up_pairs, down_index, down_pairs)

    return apply


def per_device(activations, keep, gains, up_rows, up_blocks, down_rows, down_blocks):
    up_all = gather_up(up_blocks)
    down_all = column_major_down(gather_rows(down_blocks))
    apply = make_layer(
        gains[0], up_rows[0].reshape(-1), up_all, down_rows[0].reshape(-1), down_all
    )
    places = jnp.cumsum(keep) - 1
    target = jnp.where(keep == 1, places, KEEP_DEV)
    chosen = (
        jnp.zeros((KEEP_DEV + 1,), jnp.int32)
        .at[target]
        .set(jnp.arange(keep.shape[0], dtype=jnp.int32))[:KEEP_DEV]
    )
    selected = activations[chosen]
    width = selected.shape[1]
    section = lax.axis_index(SEC)
    sections = lax.axis_size(SEC)
    pieces = 8
    group_rows = selected.shape[0] // pieces
    split = selected.reshape(pieces, group_rows, width)

    def advance(turn, held, record):
        offset = turn - section
        entry = jnp.where(section == 0, split[jnp.minimum(turn, pieces - 1)], held)
        active = (offset >= 0) & (offset < pieces)
        result = lax.cond(active, apply, jnp.zeros_like, entry)
        slot = jnp.clip(offset, 0, pieces - 1)
        current = lax.dynamic_index_in_dim(record, slot, 0, keepdims=False)
        updated = jnp.where(active, result, current)
        record = lax.dynamic_update_index_in_dim(record, updated, slot, 0)
        return (result, record)

    def turn_step(turn, carry):
        held, record = carry
        result, record = advance(turn, held, record)
        held = from_behind(result, SEC, 1)
        return (held, record)

    turns = sections + pieces - 1
    held, record = lax.fori_loop(0, turns, turn_step, (split[0], split))
    final = record.reshape(selected.shape[0], width)
    merged = activations.at[chosen].set(final)
    return merged[None]


def solution(mesh):
    zh = 4
    yc = mesh.shape["fsdp"] // zh
    zl = 2
    xs = mesh.shape["section"] // zl
    devices = mesh.devices.reshape(zl, xs, zh, yc // 2, 2)
    fine = Mesh(devices, ("zl", "x", "zh", "y", "c"))
    return jax.shard_map(
        per_device,
        mesh=fine,
        in_specs=(
            P(FS, None),
            P(FS),
            P(SEC, None),
            P(SEC, None, None),
            P(SEC, FS, None),
            P(SEC, None, None),
            P(SEC, FS, None),
        ),
        out_specs=P(SEC, FS, None),
        check_vma=False,
    )
```

```python
import jax
import jax.numpy as jnp
from jax import lax
from jax.experimental import pallas as pl
from jax.experimental.pallas import tpu as pltpu
from jax.sharding import Mesh
from jax.sharding import PartitionSpec as P

BLK = 64
UP_DEPTH = 2
DOWN_DEPTH = 2
KEEP_DEV = 128

SEC = ("zl", "x")
FS = ("zh", "y", "c")


def from_behind(value, axis, steps):
    count = lax.axis_size(axis)
    initial, last = (max(0, -steps), min(count, count - steps))
    return lax.ppermute(value, axis, [(source, source + steps) for source in range(initial, last)])


def exchange_zh(part):
    count = lax.axis_size("zh")
    own = lax.axis_index("zh")
    got = [part]
    for shift in range(1, count):
        got.append(lax.ppermute(part, "zh", [(i, (i + shift) % count) for i in range(count)]))
    stacked = jnp.stack(got)
    order = (own - jnp.arange(count, dtype=jnp.int32)) % count
    return jnp.take(stacked, order, axis=0)


def gather_weights(up_shard, down_shard):
    cols = up_shard.shape[1] // UP_DEPTH
    up_part = up_shard.reshape(cols, UP_DEPTH, BLK, BLK).transpose(0, 3, 1, 2)
    up_part = up_part.reshape(cols * BLK, UP_DEPTH * BLK)
    down_part = down_shard.reshape(down_shard.shape[1] * 32, 128)
    split = up_part.shape[0]
    full = exchange_zh(jnp.concatenate([up_part, down_part], axis=0))
    up_full = lax.all_gather(full[:, :split], ("y", "c"), axis=1, tiled=True)
    down_full = lax.all_gather(full[:, split:], ("y", "c"), axis=1, tiled=True)
    return up_full.reshape(-1, BLK, UP_DEPTH * BLK), down_full.reshape(-1, 4096)


LANE = 128
NT = (((1,), (1,)), ((), ()))


def _gelu(v):
    return 0.5 * v * (1.0 + jnp.tanh(0.7978845608028654 * (v + 0.044715 * (v * v * v))))


def _pick(s_ref, a, b, lane):
    left = s_ref[a % 2, (a + 1) // 2]
    right = s_ref[1 - b % 2, b // 2]
    return jnp.where(lane < BLK, left, right)


def _shifted(prev, cur):
    lane = lax.broadcasted_iota(jnp.int32, cur.shape, 1)
    return jnp.where(lane < BLK, pltpu.roll(prev, BLK, 1), pltpu.roll(cur, BLK, 1))


UP_CHUNKS = 4
DOWN_CHUNKS = 2


def _layer_kernel(up_idx, dn_idx, x_ref, g_ref, wu_hbm, wd_hbm, o_ref, sx_ref, sh_ref, wu_ref, wd_ref, sems):
    count, width = x_ref.shape
    pairs_in = width // LANE
    pairs_hid = wu_ref.shape[0]
    up_step = pairs_hid // UP_CHUNKS
    down_step = pairs_in // DOWN_CHUNKS
    copies = []
    for k in range(UP_CHUNKS):
        part = pl.ds(k * up_step, up_step)
        copies.append(pltpu.make_async_copy(wu_hbm.at[part], wu_ref.at[part], sems.at[k]))
    for k in range(DOWN_CHUNKS):
        part = pl.ds(k * down_step, down_step)
        copies.append(pltpu.make_async_copy(wd_hbm.at[part], wd_ref.at[part], sems.at[UP_CHUNKS + k]))
    for copy in copies:
        copy.start()
    x = x_ref[...].astype(jnp.float32)
    scale = lax.rsqrt(jnp.mean(x * x, axis=1, keepdims=True) + 1e-05)
    zero = jnp.zeros((count, LANE), jnp.bfloat16)
    prev = zero
    for p in range(pairs_in):
        cur = (x[:, p * LANE:(p + 1) * LANE] * scale * g_ref[:, p * LANE:(p + 1) * LANE]).astype(jnp.bfloat16)
        sx_ref[0, p] = cur
        sx_ref[1, p] = _shifted(prev, cur)
        prev = cur
    sx_ref[0, pairs_in] = zero
    sx_ref[1, pairs_in] = _shifted(prev, zero)
    lane = lax.broadcasted_iota(jnp.int32, (count, LANE), 1)

    def up(cp, prev):
        c0 = 2 * cp
        l0 = _pick(sx_ref, up_idx[2 * c0], up_idx[2 * c0 + 1], lane)
        l1 = _pick(sx_ref, up_idx[2 * c0 + 2], up_idx[2 * c0 + 3], lane)
        s = lax.dot_general(l0, wu_ref[cp, 0], NT, preferred_element_type=jnp.float32)
        s = s + lax.dot_general(l1, wu_ref[cp, 1], NT, preferred_element_type=jnp.float32)
        cur = _gelu(s).astype(jnp.bfloat16)
        sh_ref[0, cp] = cur
        sh_ref[1, cp] = _shifted(prev, cur)
        return cur

    last = zero
    for k in range(UP_CHUNKS):
        copies[k].wait()
        last = lax.fori_loop(k * up_step, (k + 1) * up_step, up, last, unroll=8)
    sh_ref[0, pairs_hid] = zero
    sh_ref[1, pairs_hid] = _shifted(last, zero)

    for cp in range(pairs_in):
        if cp % down_step == 0:
            copies[UP_CHUNKS + cp // down_step].wait()
        c0 = 2 * cp
        l0 = _pick(sh_ref, dn_idx[2 * c0], dn_idx[2 * c0 + 1], lane)
        l1 = _pick(sh_ref, dn_idx[2 * c0 + 2], dn_idx[2 * c0 + 3], lane)
        s = lax.dot_general(l0, wd_ref[cp, 0], NT, preferred_element_type=jnp.float32)
        s = s + lax.dot_general(l1, wd_ref[cp, 1], NT, preferred_element_type=jnp.float32)
        o_ref[:, cp * LANE:(cp + 1) * LANE] = (x[:, cp * LANE:(cp + 1) * LANE] + s).astype(jnp.bfloat16)


def pad_pairs(wt):
    cols = wt.shape[0]
    w = wt.reshape(cols // 2, 2, BLK, LANE)
    z = jnp.zeros_like(w[:, :1])
    first = jnp.concatenate([w[:, :1], z], axis=2)
    second = jnp.concatenate([z, w[:, 1:]], axis=2)
    return jnp.concatenate([first, second], axis=1)


def layer(x, gain_row, up_idx, wu_p, dn_idx, wd_p):
    count, width = x.shape
    pairs_in = width // LANE
    pairs_hid = wu_p.shape[0]
    return pl.pallas_call(
        _layer_kernel,
        out_shape=jax.ShapeDtypeStruct((count, width), jnp.bfloat16),
        grid_spec=pltpu.PrefetchScalarGridSpec(
            num_scalar_prefetch=2,
            grid=(1,),
            in_specs=[
                pl.BlockSpec((count, width), lambda i, u, d: (0, 0)),
                pl.BlockSpec((1, width), lambda i, u, d: (0, 0)),
                pl.BlockSpec(memory_space=pl.ANY),
                pl.BlockSpec(memory_space=pl.ANY),
            ],
            out_specs=pl.BlockSpec((count, width), lambda i, u, d: (0, 0)),
            scratch_shapes=[
                pltpu.VMEM((2, pairs_in + 1, count, LANE), jnp.bfloat16),
                pltpu.VMEM((2, pairs_hid + 1, count, LANE), jnp.bfloat16),
                pltpu.VMEM(wu_p.shape, wu_p.dtype),
                pltpu.VMEM(wd_p.shape, wd_p.dtype),
                pltpu.SemaphoreType.DMA((UP_CHUNKS + DOWN_CHUNKS,)),
            ],
        ),
        compiler_params=pltpu.CompilerParams(vmem_limit_bytes=40 * 1024 * 1024),
    )(up_idx, dn_idx, x, gain_row, wu_p, wd_p)


def column_major_down(rows):
    cols = rows.shape[0] // DOWN_DEPTH
    w = rows.reshape(cols, DOWN_DEPTH, BLK, BLK).transpose(0, 3, 1, 2)
    return w.reshape(cols, BLK, DOWN_DEPTH * BLK)


def make_layer(gain, up_index, up_cols, down_index, down_cols):
    gain_row = gain.astype(jnp.float32)[None, :]
    up_pairs = pad_pairs(up_cols)
    down_pairs = pad_pairs(down_cols)

    def apply(block):
        return layer(block, gain_row, up_index, up_pairs, down_index, down_pairs)

    return apply


def per_device(activations, keep, gains, up_rows, up_blocks, down_rows, down_blocks):
    up_all, down_rows_all = gather_weights(up_blocks, down_blocks)
    down_all = column_major_down(down_rows_all)
    apply = make_layer(
        gains[0], up_rows[0].reshape(-1), up_all, down_rows[0].reshape(-1), down_all
    )
    places = jnp.cumsum(keep) - 1
    target = jnp.where(keep == 1, places, KEEP_DEV)
    chosen = (
        jnp.zeros((KEEP_DEV + 1,), jnp.int32)
        .at[target]
        .set(jnp.arange(keep.shape[0], dtype=jnp.int32))[:KEEP_DEV]
    )
    selected = activations[chosen]
    width = selected.shape[1]
    section = lax.axis_index(SEC)
    sections = lax.axis_size(SEC)
    pieces = 8
    group_rows = selected.shape[0] // pieces
    split = selected.reshape(pieces, group_rows, width)

    def advance(turn, held, record):
        offset = turn - section
        entry = jnp.where(section == 0, split[jnp.minimum(turn, pieces - 1)], held)
        active = (offset >= 0) & (offset < pieces)
        result = lax.cond(active, apply, jnp.zeros_like, entry)
        slot = jnp.clip(offset, 0, pieces - 1)
        current = lax.dynamic_index_in_dim(record, slot, 0, keepdims=False)
        updated = jnp.where(active, result, current)
        record = lax.dynamic_update_index_in_dim(record, updated, slot, 0)
        return (result, record)

    def turn_step(turn, carry):
        held, record = carry
        result, record = advance(turn, held, record)
        held = from_behind(result, SEC, 1)
        return (held, record)

    turns = sections + pieces - 1
    held, record = lax.fori_loop(0, turns, turn_step, (split[0], split))
    final = record.reshape(selected.shape[0], width)
    merged = activations.at[chosen].set(final)
    return merged[None]


def solution(mesh):
    zh = 4
    yc = mesh.shape["fsdp"] // zh
    zl = 2
    xs = mesh.shape["section"] // zl
    devices = mesh.devices.reshape(zl, xs, zh, yc // 2, 2)
    fine = Mesh(devices, ("zl", "x", "zh", "y", "c"))
    return jax.shard_map(
        per_device,
        mesh=fine,
        in_specs=(
            P(FS, None),
            P(FS),
            P(SEC, None),
            P(SEC, None, None),
            P(SEC, FS, None),
            P(SEC, None, None),
            P(SEC, FS, None),
        ),
        out_specs=P(SEC, FS, None),
        check_vma=False,
    )
```

```python
import jax
import jax.numpy as jnp
from jax import lax
from jax.experimental import pallas as pl
from jax.experimental.pallas import tpu as pltpu
from jax.sharding import Mesh
from jax.sharding import PartitionSpec as P

BLK = 64
UP_DEPTH = 2
DOWN_DEPTH = 2
KEEP_DEV = 128

SEC = ("zl", "x")
FS = ("zh", "y", "c")


def from_behind(value, axis, steps):
    count = lax.axis_size(axis)
    initial, last = (max(0, -steps), min(count, count - steps))
    return lax.ppermute(value, axis, [(source, source + steps) for source in range(initial, last)])


def exchange_zh(part):
    count = lax.axis_size("zh")
    own = lax.axis_index("zh")
    got = [part]
    for shift in range(1, count):
        got.append(lax.ppermute(part, "zh", [(i, (i + shift) % count) for i in range(count)]))
    stacked = jnp.stack(got)
    order = (own - jnp.arange(count, dtype=jnp.int32)) % count
    return jnp.take(stacked, order, axis=0)


def gather_weights(up_shard, down_shard):
    cols = up_shard.shape[1] // UP_DEPTH
    up_part = up_shard.reshape(cols, UP_DEPTH, BLK, BLK).transpose(0, 3, 1, 2)
    up_part = up_part.reshape(cols * BLK, UP_DEPTH * BLK)
    down_part = down_shard.reshape(down_shard.shape[1] * 32, 128)
    split = up_part.shape[0]
    full = exchange_zh(jnp.concatenate([up_part, down_part], axis=0))
    up_full = lax.all_gather(full[:, :split], ("y", "c"), axis=1, tiled=True)
    down_full = lax.all_gather(full[:, split:], ("y", "c"), axis=1, tiled=True)
    return up_full.reshape(-1, BLK, UP_DEPTH * BLK), down_full.reshape(-1, 4096)


LANE = 128
NT = (((1,), (1,)), ((), ()))


def _gelu(v):
    return 0.5 * v * (1.0 + jnp.tanh(0.7978845608028654 * (v + 0.044715 * (v * v * v))))


def _pick(s_ref, a, b, lane):
    left = s_ref[a % 2, (a + 1) // 2]
    right = s_ref[1 - b % 2, b // 2]
    return jnp.where(lane < BLK, left, right)


def _shifted(prev, cur):
    lane = lax.broadcasted_iota(jnp.int32, cur.shape, 1)
    return jnp.where(lane < BLK, pltpu.roll(prev, BLK, 1), pltpu.roll(cur, BLK, 1))


UP_CHUNKS = 4
DOWN_CHUNKS = 2


def _layer_kernel(up_idx, dn_idx, x_ref, g_ref, wu_hbm, wd_hbm, o_ref, sx_ref, sh_ref, wu_ref, wd_ref, sems):
    count, width = x_ref.shape
    pairs_in = width // LANE
    pairs_hid = wu_ref.shape[0]
    up_step = pairs_hid // UP_CHUNKS
    down_step = pairs_in // DOWN_CHUNKS
    copies = []
    for k in range(UP_CHUNKS):
        part = pl.ds(k * up_step, up_step)
        copies.append(pltpu.make_async_copy(wu_hbm.at[part], wu_ref.at[part], sems.at[k]))
    for k in range(DOWN_CHUNKS):
        part = pl.ds(k * down_step, down_step)
        copies.append(pltpu.make_async_copy(wd_hbm.at[part], wd_ref.at[part], sems.at[UP_CHUNKS + k]))
    for copy in copies:
        copy.start()
    x = x_ref[...].astype(jnp.float32)
    scale = lax.rsqrt(jnp.mean(x * x, axis=1, keepdims=True) + 1e-05)
    zero = jnp.zeros((count, LANE), jnp.bfloat16)
    prev = zero
    for p in range(pairs_in):
        cur = (x[:, p * LANE:(p + 1) * LANE] * scale * g_ref[:, p * LANE:(p + 1) * LANE]).astype(jnp.bfloat16)
        sx_ref[0, p] = cur
        sx_ref[1, p] = _shifted(prev, cur)
        prev = cur
    sx_ref[0, pairs_in] = zero
    sx_ref[1, pairs_in] = _shifted(prev, zero)
    lane = lax.broadcasted_iota(jnp.int32, (count, LANE), 1)

    def up(cp, prev):
        c0 = 2 * cp
        l0 = _pick(sx_ref, up_idx[2 * c0], up_idx[2 * c0 + 1], lane)
        l1 = _pick(sx_ref, up_idx[2 * c0 + 2], up_idx[2 * c0 + 3], lane)
        w = wu_ref[cp]
        s0 = lax.dot_general(l0, w, NT, preferred_element_type=jnp.float32)
        s1 = lax.dot_general(l1, w, NT, preferred_element_type=jnp.float32)
        cur = _gelu(jnp.where(lane < BLK, s0, s1)).astype(jnp.bfloat16)
        sh_ref[0, cp] = cur
        sh_ref[1, cp] = _shifted(prev, cur)
        return cur

    last = zero
    for k in range(UP_CHUNKS):
        copies[k].wait()
        last = lax.fori_loop(k * up_step, (k + 1) * up_step, up, last, unroll=8)
    sh_ref[0, pairs_hid] = zero
    sh_ref[1, pairs_hid] = _shifted(last, zero)

    for cp in range(pairs_in):
        if cp % down_step == 0:
            copies[UP_CHUNKS + cp // down_step].wait()
        c0 = 2 * cp
        l0 = _pick(sh_ref, dn_idx[2 * c0], dn_idx[2 * c0 + 1], lane)
        l1 = _pick(sh_ref, dn_idx[2 * c0 + 2], dn_idx[2 * c0 + 3], lane)
        w = wd_ref[cp]
        s0 = lax.dot_general(l0, w, NT, preferred_element_type=jnp.float32)
        s1 = lax.dot_general(l1, w, NT, preferred_element_type=jnp.float32)
        s = jnp.where(lane < BLK, s0, s1)
        o_ref[:, cp * LANE:(cp + 1) * LANE] = (x[:, cp * LANE:(cp + 1) * LANE] + s).astype(jnp.bfloat16)


def as_pairs(wt):
    return wt.reshape(wt.shape[0] // 2, 2 * BLK, LANE)


def layer(x, gain_row, up_idx, wu_p, dn_idx, wd_p):
    count, width = x.shape
    pairs_in = width // LANE
    pairs_hid = wu_p.shape[0]
    return pl.pallas_call(
        _layer_kernel,
        out_shape=jax.ShapeDtypeStruct((count, width), jnp.bfloat16),
        grid_spec=pltpu.PrefetchScalarGridSpec(
            num_scalar_prefetch=2,
            grid=(1,),
            in_specs=[
                pl.BlockSpec((count, width), lambda i, u, d: (0, 0)),
                pl.BlockSpec((1, width), lambda i, u, d: (0, 0)),
                pl.BlockSpec(memory_space=pl.ANY),
                pl.BlockSpec(memory_space=pl.ANY),
            ],
            out_specs=pl.BlockSpec((count, width), lambda i, u, d: (0, 0)),
            scratch_shapes=[
                pltpu.VMEM((2, pairs_in + 1, count, LANE), jnp.bfloat16),
                pltpu.VMEM((2, pairs_hid + 1, count, LANE), jnp.bfloat16),
                pltpu.VMEM(wu_p.shape, wu_p.dtype),
                pltpu.VMEM(wd_p.shape, wd_p.dtype),
                pltpu.SemaphoreType.DMA((UP_CHUNKS + DOWN_CHUNKS,)),
            ],
        ),
        compiler_params=pltpu.CompilerParams(vmem_limit_bytes=40 * 1024 * 1024),
    )(up_idx, dn_idx, x, gain_row, wu_p, wd_p)


def column_major_down(rows):
    cols = rows.shape[0] // DOWN_DEPTH
    w = rows.reshape(cols, DOWN_DEPTH, BLK, BLK).transpose(0, 3, 1, 2)
    return w.reshape(cols, BLK, DOWN_DEPTH * BLK)


def make_layer(gain, up_index, up_cols, down_index, down_cols):
    gain_row = gain.astype(jnp.float32)[None, :]
    up_pairs = as_pairs(up_cols)
    down_pairs = as_pairs(down_cols)

    def apply(block):
        return layer(block, gain_row, up_index, up_pairs, down_index, down_pairs)

    return apply


def per_device(activations, keep, gains, up_rows, up_blocks, down_rows, down_blocks):
    up_all, down_rows_all = gather_weights(up_blocks, down_blocks)
    down_all = column_major_down(down_rows_all)
    apply = make_layer(
        gains[0], up_rows[0].reshape(-1), up_all, down_rows[0].reshape(-1), down_all
    )
    places = jnp.cumsum(keep) - 1
    target = jnp.where(keep == 1, places, KEEP_DEV)
    chosen = (
        jnp.zeros((KEEP_DEV + 1,), jnp.int32)
        .at[target]
        .set(jnp.arange(keep.shape[0], dtype=jnp.int32))[:KEEP_DEV]
    )
    selected = activations[chosen]
    width = selected.shape[1]
    section = lax.axis_index(SEC)
    sections = lax.axis_size(SEC)
    pieces = 4
    group_rows = selected.shape[0] // pieces
    split = selected.reshape(pieces, group_rows, width)

    def advance(turn, held, record):
        offset = turn - section
        entry = jnp.where(section == 0, split[jnp.minimum(turn, pieces - 1)], held)
        active = (offset >= 0) & (offset < pieces)
        result = lax.cond(active, apply, jnp.zeros_like, entry)
        slot = jnp.clip(offset, 0, pieces - 1)
        current = lax.dynamic_index_in_dim(record, slot, 0, keepdims=False)
        updated = jnp.where(active, result, current)
        record = lax.dynamic_update_index_in_dim(record, updated, slot, 0)
        return (result, record)

    def turn_step(turn, carry):
        held, record = carry
        result, record = advance(turn, held, record)
        held = from_behind(result, SEC, 1)
        return (held, record)

    turns = sections + pieces - 1
    held, record = lax.fori_loop(0, turns, turn_step, (split[0], split))
    final = record.reshape(selected.shape[0], width)
    merged = activations.at[chosen].set(final)
    return merged[None]


def solution(mesh):
    zh = 4
    yc = mesh.shape["fsdp"] // zh
    zl = 2
    xs = mesh.shape["section"] // zl
    devices = mesh.devices.reshape(zl, xs, zh, yc // 2, 2)
    fine = Mesh(devices, ("zl", "x", "zh", "y", "c"))
    return jax.shard_map(
        per_device,
        mesh=fine,
        in_specs=(
            P(FS, None),
            P(FS),
            P(SEC, None),
            P(SEC, None, None),
            P(SEC, FS, None),
            P(SEC, None, None),
            P(SEC, FS, None),
        ),
        out_specs=P(SEC, FS, None),
        check_vma=False,
    )
```

```python
import jax
import jax.numpy as jnp
from jax import lax
from jax.experimental import pallas as pl
from jax.experimental.pallas import tpu as pltpu
from jax.sharding import Mesh
from jax.sharding import PartitionSpec as P

BLK = 64
UP_DEPTH = 2
DOWN_DEPTH = 2
KEEP_DEV = 128

SEC = ("zl", "x")
FS = ("zh", "y", "c")


def from_behind(value, axis, steps):
    count = lax.axis_size(axis)
    initial, last = (max(0, -steps), min(count, count - steps))
    return lax.ppermute(value, axis, [(source, source + steps) for source in range(initial, last)])


def exchange_zh(part):
    count = lax.axis_size("zh")
    own = lax.axis_index("zh")
    got = [part]
    for shift in range(1, count):
        got.append(lax.ppermute(part, "zh", [(i, (i + shift) % count) for i in range(count)]))
    stacked = jnp.stack(got)
    order = (own - jnp.arange(count, dtype=jnp.int32)) % count
    return jnp.take(stacked, order, axis=0)


def gather_weights(up_shard, down_shard):
    cols = up_shard.shape[1] // UP_DEPTH
    up_part = up_shard.reshape(cols, UP_DEPTH, BLK, BLK).transpose(0, 3, 1, 2)
    up_part = up_part.reshape(cols * BLK, UP_DEPTH * BLK)
    down_part = down_shard.reshape(down_shard.shape[1] * 32, 128)
    split = up_part.shape[0]
    full = exchange_zh(jnp.concatenate([up_part, down_part], axis=0))
    full = lax.all_gather(full[:, None], ("y", "c"), axis=1, tiled=True)
    up_full = full[:, :, :split]
    down_full = full[:, :, split:]
    return up_full.reshape(-1, BLK, UP_DEPTH * BLK), down_full.reshape(-1, 4096)


LANE = 128
NT = (((1,), (1,)), ((), ()))


def _gelu(v):
    return 0.5 * v * (1.0 + jnp.tanh(0.7978845608028654 * (v + 0.044715 * (v * v * v))))


def _pick(s_ref, a, b, lane):
    left = s_ref[a % 2, (a + 1) // 2]
    right = s_ref[1 - b % 2, b // 2]
    return jnp.where(lane < BLK, left, right)


def _shifted(prev, cur):
    lane = lax.broadcasted_iota(jnp.int32, cur.shape, 1)
    return jnp.where(lane < BLK, pltpu.roll(prev, BLK, 1), pltpu.roll(cur, BLK, 1))


UP_CHUNKS = 4
DOWN_CHUNKS = 2


def _layer_kernel(up_idx, dn_idx, x_ref, g_ref, wu_hbm, wd_hbm, o_ref, sx_ref, sh_ref, wu_ref, wd_ref, sems):
    count, width = x_ref.shape
    pairs_in = width // LANE
    pairs_hid = wu_ref.shape[0]
    up_step = pairs_hid // UP_CHUNKS
    down_step = pairs_in // DOWN_CHUNKS
    copies = []
    for k in range(UP_CHUNKS):
        part = pl.ds(k * up_step, up_step)
        copies.append(pltpu.make_async_copy(wu_hbm.at[part], wu_ref.at[part], sems.at[k]))
    for k in range(DOWN_CHUNKS):
        part = pl.ds(k * down_step, down_step)
        copies.append(pltpu.make_async_copy(wd_hbm.at[part], wd_ref.at[part], sems.at[UP_CHUNKS + k]))
    for copy in copies:
        copy.start()
    x = x_ref[...].astype(jnp.float32)
    scale = lax.rsqrt(jnp.mean(x * x, axis=1, keepdims=True) + 1e-05)
    zero = jnp.zeros((count, LANE), jnp.bfloat16)
    prev = zero
    for p in range(pairs_in):
        cur = (x[:, p * LANE:(p + 1) * LANE] * scale * g_ref[:, p * LANE:(p + 1) * LANE]).astype(jnp.bfloat16)
        sx_ref[0, p] = cur
        sx_ref[1, p] = _shifted(prev, cur)
        prev = cur
    sx_ref[0, pairs_in] = zero
    sx_ref[1, pairs_in] = _shifted(prev, zero)
    lane = lax.broadcasted_iota(jnp.int32, (count, LANE), 1)

    def up(cp, prev):
        c0 = 2 * cp
        l0 = _pick(sx_ref, up_idx[2 * c0], up_idx[2 * c0 + 1], lane)
        l1 = _pick(sx_ref, up_idx[2 * c0 + 2], up_idx[2 * c0 + 3], lane)
        w = wu_ref[cp]
        s0 = lax.dot_general(l0, w, NT, preferred_element_type=jnp.float32)
        s1 = lax.dot_general(l1, w, NT, preferred_element_type=jnp.float32)
        cur = _gelu(jnp.where(lane < BLK, s0, s1)).astype(jnp.bfloat16)
        sh_ref[0, cp] = cur
        sh_ref[1, cp] = _shifted(prev, cur)
        return cur

    last = zero
    for k in range(UP_CHUNKS):
        copies[k].wait()
        last = lax.fori_loop(k * up_step, (k + 1) * up_step, up, last, unroll=8)
    sh_ref[0, pairs_hid] = zero
    sh_ref[1, pairs_hid] = _shifted(last, zero)

    for cp in range(pairs_in):
        if cp % down_step == 0:
            copies[UP_CHUNKS + cp // down_step].wait()
        c0 = 2 * cp
        l0 = _pick(sh_ref, dn_idx[2 * c0], dn_idx[2 * c0 + 1], lane)
        l1 = _pick(sh_ref, dn_idx[2 * c0 + 2], dn_idx[2 * c0 + 3], lane)
        w = wd_ref[cp]
        s0 = lax.dot_general(l0, w, NT, preferred_element_type=jnp.float32)
        s1 = lax.dot_general(l1, w, NT, preferred_element_type=jnp.float32)
        s = jnp.where(lane < BLK, s0, s1)
        o_ref[:, cp * LANE:(cp + 1) * LANE] = (x[:, cp * LANE:(cp + 1) * LANE] + s).astype(jnp.bfloat16)


def as_pairs(wt):
    return wt.reshape(wt.shape[0] // 2, 2 * BLK, LANE)


def layer(x, gain_row, up_idx, wu_p, dn_idx, wd_p):
    count, width = x.shape
    pairs_in = width // LANE
    pairs_hid = wu_p.shape[0]
    return pl.pallas_call(
        _layer_kernel,
        out_shape=jax.ShapeDtypeStruct((count, width), jnp.bfloat16),
        grid_spec=pltpu.PrefetchScalarGridSpec(
            num_scalar_prefetch=2,
            grid=(1,),
            in_specs=[
                pl.BlockSpec((count, width), lambda i, u, d: (0, 0)),
                pl.BlockSpec((1, width), lambda i, u, d: (0, 0)),
                pl.BlockSpec(memory_space=pl.ANY),
                pl.BlockSpec(memory_space=pl.ANY),
            ],
            out_specs=pl.BlockSpec((count, width), lambda i, u, d: (0, 0)),
            scratch_shapes=[
                pltpu.VMEM((2, pairs_in + 1, count, LANE), jnp.bfloat16),
                pltpu.VMEM((2, pairs_hid + 1, count, LANE), jnp.bfloat16),
                pltpu.VMEM(wu_p.shape, wu_p.dtype),
                pltpu.VMEM(wd_p.shape, wd_p.dtype),
                pltpu.SemaphoreType.DMA((UP_CHUNKS + DOWN_CHUNKS,)),
            ],
        ),
        compiler_params=pltpu.CompilerParams(vmem_limit_bytes=40 * 1024 * 1024),
    )(up_idx, dn_idx, x, gain_row, wu_p, wd_p)


def column_major_down(rows):
    cols = rows.shape[0] // DOWN_DEPTH
    w = rows.reshape(cols, DOWN_DEPTH, BLK, BLK).transpose(0, 3, 1, 2)
    return w.reshape(cols, BLK, DOWN_DEPTH * BLK)


def make_layer(gain, up_index, up_cols, down_index, down_cols):
    gain_row = gain.astype(jnp.float32)[None, :]
    up_pairs = as_pairs(up_cols)
    down_pairs = as_pairs(down_cols)

    def apply(block):
        return layer(block, gain_row, up_index, up_pairs, down_index, down_pairs)

    return apply


def per_device(activations, keep, gains, up_rows, up_blocks, down_rows, down_blocks):
    up_all, down_rows_all = gather_weights(up_blocks, down_blocks)
    down_all = column_major_down(down_rows_all)
    apply = make_layer(
        gains[0], up_rows[0].reshape(-1), up_all, down_rows[0].reshape(-1), down_all
    )
    places = jnp.cumsum(keep) - 1
    target = jnp.where(keep == 1, places, KEEP_DEV)
    chosen = (
        jnp.zeros((KEEP_DEV + 1,), jnp.int32)
        .at[target]
        .set(jnp.arange(keep.shape[0], dtype=jnp.int32))[:KEEP_DEV]
    )
    selected = activations[chosen]
    width = selected.shape[1]
    section = lax.axis_index(SEC)
    sections = lax.axis_size(SEC)
    pieces = 4
    group_rows = selected.shape[0] // pieces
    split = selected.reshape(pieces, group_rows, width)

    def advance(turn, held, record):
        offset = turn - section
        entry = jnp.where(section == 0, split[jnp.minimum(turn, pieces - 1)], held)
        active = (offset >= 0) & (offset < pieces)
        result = lax.cond(active, apply, jnp.zeros_like, entry)
        slot = jnp.clip(offset, 0, pieces - 1)
        current = lax.dynamic_index_in_dim(record, slot, 0, keepdims=False)
        updated = jnp.where(active, result, current)
        record = lax.dynamic_update_index_in_dim(record, updated, slot, 0)
        return (result, record)

    def turn_step(turn, carry):
        held, record = carry
        result, record = advance(turn, held, record)
        held = from_behind(result, SEC, 1)
        return (held, record)

    turns = sections + pieces - 1
    held, record = lax.fori_loop(0, turns, turn_step, (split[0], split))
    final = record.reshape(selected.shape[0], width)
    merged = activations.at[chosen].set(final)
    return merged[None]


def solution(mesh):
    zh = 4
    yc = mesh.shape["fsdp"] // zh
    zl = 2
    xs = mesh.shape["section"] // zl
    devices = mesh.devices.reshape(zl, xs, zh, yc // 2, 2)
    fine = Mesh(devices, ("zl", "x", "zh", "y", "c"))
    return jax.shard_map(
        per_device,
        mesh=fine,
        in_specs=(
            P(FS, None),
            P(FS),
            P(SEC, None),
            P(SEC, None, None),
            P(SEC, FS, None),
            P(SEC, None, None),
            P(SEC, FS, None),
        ),
        out_specs=P(SEC, FS, None),
        check_vma=False,
    )
```

```python
import jax
import jax.numpy as jnp
from jax import lax
from jax.experimental import pallas as pl
from jax.experimental.pallas import tpu as pltpu
from jax.sharding import Mesh
from jax.sharding import PartitionSpec as P

BLK = 64
UP_DEPTH = 2
DOWN_DEPTH = 2
KEEP_DEV = 128

SEC = ("zl", "x")
FS = ("zh", "y", "c")


def from_behind(value, axis, steps):
    count = lax.axis_size(axis)
    initial, last = (max(0, -steps), min(count, count - steps))
    return lax.ppermute(value, axis, [(source, source + steps) for source in range(initial, last)])


def exchange_zh(part):
    count = lax.axis_size("zh")
    own = lax.axis_index("zh")
    got = [part]
    for shift in range(1, count):
        got.append(lax.ppermute(part, "zh", [(i, (i + shift) % count) for i in range(count)]))
    stacked = jnp.stack(got)
    order = (own - jnp.arange(count, dtype=jnp.int32)) % count
    return jnp.take(stacked, order, axis=0)


def gather_weights(up_shard, down_shard):
    cols = up_shard.shape[1] // UP_DEPTH
    up_part = up_shard.reshape(cols, UP_DEPTH, BLK, BLK).transpose(0, 3, 1, 2)
    up_part = up_part.reshape(cols * BLK, UP_DEPTH * BLK)
    down_part = down_shard.reshape(down_shard.shape[1] * 32, 128)
    split = up_part.shape[0]
    full = exchange_zh(jnp.concatenate([up_part, down_part], axis=0))
    full = lax.all_gather(full[:, None], ("y", "c"), axis=1, tiled=True)
    up_full = full[:, :, :split]
    down_full = full[:, :, split:]
    return up_full.reshape(-1, BLK, UP_DEPTH * BLK), down_full.reshape(-1, 4096)


LANE = 128
NT = (((1,), (1,)), ((), ()))


def _gelu(v):
    return 0.5 * v * (1.0 + jnp.tanh(0.7978845608028654 * (v + 0.044715 * (v * v * v))))


def _pick(s_ref, a, b, lane):
    left = s_ref[a % 2, (a + 1) // 2]
    right = s_ref[1 - b % 2, b // 2]
    return jnp.where(lane < BLK, left, right)


def _shifted(prev, cur):
    lane = lax.broadcasted_iota(jnp.int32, cur.shape, 1)
    return jnp.where(lane < BLK, pltpu.roll(prev, BLK, 1), pltpu.roll(cur, BLK, 1))


UP_CHUNKS = 4
DOWN_CHUNKS = 2


def _layer_kernel(up_idx, dn_idx, flags, xs_ref, xh_ref, g_ref, wu_hbm, wd_hbm, rec_hbm, o_ref, r_ref,
                  sx_ref, sh_ref, wu_ref, wd_ref, sems):
    del rec_hbm
    count, width = xh_ref.shape
    pairs_in = width // LANE
    pairs_hid = wu_ref.shape[0]
    up_step = pairs_hid // UP_CHUNKS
    down_step = pairs_in // DOWN_CHUNKS
    copies = []
    for k in range(UP_CHUNKS):
        part = pl.ds(k * up_step, up_step)
        copies.append(pltpu.make_async_copy(wu_hbm.at[part], wu_ref.at[part], sems.at[k]))
    for k in range(DOWN_CHUNKS):
        part = pl.ds(k * down_step, down_step)
        copies.append(pltpu.make_async_copy(wd_hbm.at[part], wd_ref.at[part], sems.at[UP_CHUNKS + k]))
    for copy in copies:
        copy.start()
    first = jnp.full((count, width), flags[0], jnp.int32) == 1
    x = jnp.where(first, xs_ref[...], xh_ref[...]).astype(jnp.float32)
    scale = lax.rsqrt(jnp.mean(x * x, axis=1, keepdims=True) + 1e-05)
    zero = jnp.zeros((count, LANE), jnp.bfloat16)
    prev = zero
    for p in range(pairs_in):
        cur = (x[:, p * LANE:(p + 1) * LANE] * scale * g_ref[:, p * LANE:(p + 1) * LANE]).astype(jnp.bfloat16)
        sx_ref[0, p] = cur
        sx_ref[1, p] = _shifted(prev, cur)
        prev = cur
    sx_ref[0, pairs_in] = zero
    sx_ref[1, pairs_in] = _shifted(prev, zero)
    lane = lax.broadcasted_iota(jnp.int32, (count, LANE), 1)

    def up(cp, prev):
        c0 = 2 * cp
        l0 = _pick(sx_ref, up_idx[2 * c0], up_idx[2 * c0 + 1], lane)
        l1 = _pick(sx_ref, up_idx[2 * c0 + 2], up_idx[2 * c0 + 3], lane)
        w = wu_ref[cp]
        s0 = lax.dot_general(l0, w, NT, preferred_element_type=jnp.float32)
        s1 = lax.dot_general(l1, w, NT, preferred_element_type=jnp.float32)
        cur = _gelu(jnp.where(lane < BLK, s0, s1)).astype(jnp.bfloat16)
        sh_ref[0, cp] = cur
        sh_ref[1, cp] = _shifted(prev, cur)
        return cur

    last = zero
    for k in range(UP_CHUNKS):
        copies[k].wait()
        last = lax.fori_loop(k * up_step, (k + 1) * up_step, up, last, unroll=8)
    sh_ref[0, pairs_hid] = zero
    sh_ref[1, pairs_hid] = _shifted(last, zero)

    for cp in range(pairs_in):
        if cp % down_step == 0:
            copies[UP_CHUNKS + cp // down_step].wait()
        c0 = 2 * cp
        l0 = _pick(sh_ref, dn_idx[2 * c0], dn_idx[2 * c0 + 1], lane)
        l1 = _pick(sh_ref, dn_idx[2 * c0 + 2], dn_idx[2 * c0 + 3], lane)
        w = wd_ref[cp]
        s0 = lax.dot_general(l0, w, NT, preferred_element_type=jnp.float32)
        s1 = lax.dot_general(l1, w, NT, preferred_element_type=jnp.float32)
        s = jnp.where(lane < BLK, s0, s1)
        out = (x[:, cp * LANE:(cp + 1) * LANE] + s).astype(jnp.bfloat16)
        o_ref[:, cp * LANE:(cp + 1) * LANE] = out
        r_ref[:, cp * LANE:(cp + 1) * LANE] = out


def as_pairs(wt):
    return wt.reshape(wt.shape[0] // 2, 2 * BLK, LANE)


def layer(flags, split, held, record, gain_row, up_idx, wu_p, dn_idx, wd_p):
    count, width = held.shape
    pairs_in = width // LANE
    pairs_hid = wu_p.shape[0]
    return pl.pallas_call(
        _layer_kernel,
        out_shape=(
            jax.ShapeDtypeStruct((count, width), jnp.bfloat16),
            jax.ShapeDtypeStruct(record.shape, record.dtype),
        ),
        grid_spec=pltpu.PrefetchScalarGridSpec(
            num_scalar_prefetch=3,
            grid=(1,),
            in_specs=[
                pl.BlockSpec((None, count, width), lambda i, u, d, f: (f[1], 0, 0)),
                pl.BlockSpec((count, width), lambda i, u, d, f: (0, 0)),
                pl.BlockSpec((1, width), lambda i, u, d, f: (0, 0)),
                pl.BlockSpec(memory_space=pl.ANY),
                pl.BlockSpec(memory_space=pl.ANY),
                pl.BlockSpec(memory_space=pl.ANY),
            ],
            out_specs=[
                pl.BlockSpec((count, width), lambda i, u, d, f: (0, 0)),
                pl.BlockSpec((None, count, width), lambda i, u, d, f: (f[2], 0, 0)),
            ],
            scratch_shapes=[
                pltpu.VMEM((2, pairs_in + 1, count, LANE), jnp.bfloat16),
                pltpu.VMEM((2, pairs_hid + 1, count, LANE), jnp.bfloat16),
                pltpu.VMEM(wu_p.shape, wu_p.dtype),
                pltpu.VMEM(wd_p.shape, wd_p.dtype),
                pltpu.SemaphoreType.DMA((UP_CHUNKS + DOWN_CHUNKS,)),
            ],
        ),
        input_output_aliases={8: 1},
        compiler_params=pltpu.CompilerParams(vmem_limit_bytes=40 * 1024 * 1024),
    )(up_idx, dn_idx, flags, split, held, gain_row, wu_p, wd_p, record)


def column_major_down(rows):
    cols = rows.shape[0] // DOWN_DEPTH
    w = rows.reshape(cols, DOWN_DEPTH, BLK, BLK).transpose(0, 3, 1, 2)
    return w.reshape(cols, BLK, DOWN_DEPTH * BLK)


def make_layer(gain, up_index, up_cols, down_index, down_cols):
    gain_row = gain.astype(jnp.float32)[None, :]
    up_pairs = as_pairs(up_cols)
    down_pairs = as_pairs(down_cols)

    def apply(flags, split, held, record):
        return layer(flags, split, held, record, gain_row, up_index, up_pairs, down_index, down_pairs)

    return apply


def per_device(activations, keep, gains, up_rows, up_blocks, down_rows, down_blocks):
    up_all, down_rows_all = gather_weights(up_blocks, down_blocks)
    down_all = column_major_down(down_rows_all)
    apply = make_layer(
        gains[0], up_rows[0].reshape(-1), up_all, down_rows[0].reshape(-1), down_all
    )
    places = jnp.cumsum(keep) - 1
    target = jnp.where(keep == 1, places, KEEP_DEV)
    chosen = (
        jnp.zeros((KEEP_DEV + 1,), jnp.int32)
        .at[target]
        .set(jnp.arange(keep.shape[0], dtype=jnp.int32))[:KEEP_DEV]
    )
    selected = activations[chosen]
    width = selected.shape[1]
    section = lax.axis_index(SEC)
    sections = lax.axis_size(SEC)
    pieces = 4
    group_rows = selected.shape[0] // pieces
    split = selected.reshape(pieces, group_rows, width)

    def advance(turn, held, record):
        offset = turn - section
        active = (offset >= 0) & (offset < pieces)
        flags = jnp.stack(
            [(section == 0).astype(jnp.int32), jnp.minimum(turn, pieces - 1), jnp.clip(offset, 0, pieces - 1)]
        ).astype(jnp.int32)

        def run(held, record):
            return apply(flags, split, held, record)

        def skip(held, record):
            return held, record

        return lax.cond(active, run, skip, held, record)

    def turn_step(turn, carry):
        held, record = carry
        result, record = advance(turn, held, record)
        held = from_behind(result, SEC, 1)
        return (held, record)

    turns = sections + pieces - 1
    held, record = lax.fori_loop(0, turns, turn_step, (split[0], split))
    final = record.reshape(selected.shape[0], width)
    merged = activations.at[chosen].set(final)
    return merged[None]


def solution(mesh):
    zh = 4
    yc = mesh.shape["fsdp"] // zh
    zl = 2
    xs = mesh.shape["section"] // zl
    devices = mesh.devices.reshape(zl, xs, zh, yc // 2, 2)
    fine = Mesh(devices, ("zl", "x", "zh", "y", "c"))
    return jax.shard_map(
        per_device,
        mesh=fine,
        in_specs=(
            P(FS, None),
            P(FS),
            P(SEC, None),
            P(SEC, None, None),
            P(SEC, FS, None),
            P(SEC, None, None),
            P(SEC, FS, None),
        ),
        out_specs=P(SEC, FS, None),
        check_vma=False,
    )
```

```python
import jax
import jax.numpy as jnp
from jax import lax
from jax.experimental import pallas as pl
from jax.experimental.pallas import tpu as pltpu
from jax.sharding import Mesh
from jax.sharding import PartitionSpec as P

BLK = 64
UP_DEPTH = 2
DOWN_DEPTH = 2
KEEP_DEV = 128

SEC = ("zl", "x")
FS = ("zh", "y", "c")


def from_behind(value, axis, steps):
    count = lax.axis_size(axis)
    initial, last = (max(0, -steps), min(count, count - steps))
    return lax.ppermute(value, axis, [(source, source + steps) for source in range(initial, last)])


def exchange_zh(part):
    count = lax.axis_size("zh")
    own = lax.axis_index("zh")
    got = [part]
    for shift in range(1, count):
        got.append(lax.ppermute(part, "zh", [(i, (i + shift) % count) for i in range(count)]))
    stacked = jnp.stack(got)
    order = (own - jnp.arange(count, dtype=jnp.int32)) % count
    return jnp.take(stacked, order, axis=0)


def gather_weights(up_shard, down_shard):
    cols = up_shard.shape[1] // UP_DEPTH
    up_part = up_shard.reshape(cols, UP_DEPTH, BLK, BLK).transpose(0, 3, 1, 2)
    up_part = up_part.reshape(cols * BLK, UP_DEPTH * BLK)
    count = down_shard.shape[1]
    blocks = down_shard.reshape(count, BLK, BLK).transpose(0, 2, 1)
    zeros = jnp.zeros_like(blocks)
    first = lax.axis_index(FS) * count + jnp.arange(count, dtype=jnp.int32)
    odd = (first % DOWN_DEPTH == 1)[:, None, None]
    placed = jnp.where(odd, jnp.concatenate([zeros, blocks], axis=2), jnp.concatenate([blocks, zeros], axis=2))
    down_part = placed.reshape(count * BLK, DOWN_DEPTH * BLK)
    split = up_part.shape[0]
    full = exchange_zh(jnp.concatenate([up_part, down_part], axis=0))
    full = lax.all_gather(full[:, None], ("y", "c"), axis=1, tiled=True)
    up_full = full[:, :, :split].reshape(-1, BLK, UP_DEPTH * BLK)
    down_full = full[:, :, split:].reshape(-1, DOWN_DEPTH, BLK, DOWN_DEPTH * BLK)
    return up_full, down_full[:, 0] + down_full[:, 1]


LANE = 128
NT = (((1,), (1,)), ((), ()))


def _gelu(v):
    return 0.5 * v * (1.0 + jnp.tanh(0.7978845608028654 * (v + 0.044715 * (v * v * v))))


def _pick(s_ref, a, b, lane):
    left = s_ref[a % 2, (a + 1) // 2]
    right = s_ref[1 - b % 2, b // 2]
    return jnp.where(lane < BLK, left, right)


def _shifted(prev, cur):
    lane = lax.broadcasted_iota(jnp.int32, cur.shape, 1)
    return jnp.where(lane < BLK, pltpu.roll(prev, BLK, 1), pltpu.roll(cur, BLK, 1))


UP_CHUNKS = 4
DOWN_CHUNKS = 2


def _layer_kernel(up_idx, dn_idx, x_ref, g_ref, wu_hbm, wd_hbm, o_ref, sx_ref, sh_ref, wu_ref, wd_ref, sems):
    count, width = x_ref.shape
    pairs_in = width // LANE
    pairs_hid = wu_ref.shape[0]
    up_step = pairs_hid // UP_CHUNKS
    down_step = pairs_in // DOWN_CHUNKS
    copies = []
    for k in range(UP_CHUNKS):
        part = pl.ds(k * up_step, up_step)
        copies.append(pltpu.make_async_copy(wu_hbm.at[part], wu_ref.at[part], sems.at[k]))
    for k in range(DOWN_CHUNKS):
        part = pl.ds(k * down_step, down_step)
        copies.append(pltpu.make_async_copy(wd_hbm.at[part], wd_ref.at[part], sems.at[UP_CHUNKS + k]))
    for copy in copies:
        copy.start()
    x = x_ref[...].astype(jnp.float32)
    scale = lax.rsqrt(jnp.mean(x * x, axis=1, keepdims=True) + 1e-05)
    zero = jnp.zeros((count, LANE), jnp.bfloat16)
    prev = zero
    for p in range(pairs_in):
        cur = (x[:, p * LANE:(p + 1) * LANE] * scale * g_ref[:, p * LANE:(p + 1) * LANE]).astype(jnp.bfloat16)
        sx_ref[0, p] = cur
        sx_ref[1, p] = _shifted(prev, cur)
        prev = cur
    sx_ref[0, pairs_in] = zero
    sx_ref[1, pairs_in] = _shifted(prev, zero)
    lane = lax.broadcasted_iota(jnp.int32, (count, LANE), 1)

    def up(cp, prev):
        c0 = 2 * cp
        l0 = _pick(sx_ref, up_idx[2 * c0], up_idx[2 * c0 + 1], lane)
        l1 = _pick(sx_ref, up_idx[2 * c0 + 2], up_idx[2 * c0 + 3], lane)
        w = wu_ref[cp]
        s0 = lax.dot_general(l0, w, NT, preferred_element_type=jnp.float32)
        s1 = lax.dot_general(l1, w, NT, preferred_element_type=jnp.float32)
        cur = _gelu(jnp.where(lane < BLK, s0, s1)).astype(jnp.bfloat16)
        sh_ref[0, cp] = cur
        sh_ref[1, cp] = _shifted(prev, cur)
        return cur

    last = zero
    for k in range(UP_CHUNKS):
        copies[k].wait()
        last = lax.fori_loop(k * up_step, (k + 1) * up_step, up, last, unroll=8)
    sh_ref[0, pairs_hid] = zero
    sh_ref[1, pairs_hid] = _shifted(last, zero)

    for cp in range(pairs_in):
        if cp % down_step == 0:
            copies[UP_CHUNKS + cp // down_step].wait()
        c0 = 2 * cp
        l0 = _pick(sh_ref, dn_idx[2 * c0], dn_idx[2 * c0 + 1], lane)
        l1 = _pick(sh_ref, dn_idx[2 * c0 + 2], dn_idx[2 * c0 + 3], lane)
        w = wd_ref[cp]
        s0 = lax.dot_general(l0, w, NT, preferred_element_type=jnp.float32)
        s1 = lax.dot_general(l1, w, NT, preferred_element_type=jnp.float32)
        s = jnp.where(lane < BLK, s0, s1)
        o_ref[:, cp * LANE:(cp + 1) * LANE] = (x[:, cp * LANE:(cp + 1) * LANE] + s).astype(jnp.bfloat16)


def as_pairs(wt):
    return wt.reshape(wt.shape[0] // 2, 2 * BLK, LANE)


def layer(x, gain_row, up_idx, wu_p, dn_idx, wd_p):
    count, width = x.shape
    pairs_in = width // LANE
    pairs_hid = wu_p.shape[0]
    return pl.pallas_call(
        _layer_kernel,
        out_shape=jax.ShapeDtypeStruct((count, width), jnp.bfloat16),
        grid_spec=pltpu.PrefetchScalarGridSpec(
            num_scalar_prefetch=2,
            grid=(1,),
            in_specs=[
                pl.BlockSpec((count, width), lambda i, u, d: (0, 0)),
                pl.BlockSpec((1, width), lambda i, u, d: (0, 0)),
                pl.BlockSpec(memory_space=pl.ANY),
                pl.BlockSpec(memory_space=pl.ANY),
            ],
            out_specs=pl.BlockSpec((count, width), lambda i, u, d: (0, 0)),
            scratch_shapes=[
                pltpu.VMEM((2, pairs_in + 1, count, LANE), jnp.bfloat16),
                pltpu.VMEM((2, pairs_hid + 1, count, LANE), jnp.bfloat16),
                pltpu.VMEM(wu_p.shape, wu_p.dtype),
                pltpu.VMEM(wd_p.shape, wd_p.dtype),
                pltpu.SemaphoreType.DMA((UP_CHUNKS + DOWN_CHUNKS,)),
            ],
        ),
        compiler_params=pltpu.CompilerParams(vmem_limit_bytes=40 * 1024 * 1024),
    )(up_idx, dn_idx, x, gain_row, wu_p, wd_p)


def make_layer(gain, up_index, up_cols, down_index, down_cols):
    gain_row = gain.astype(jnp.float32)[None, :]
    up_pairs = as_pairs(up_cols)
    down_pairs = as_pairs(down_cols)

    def apply(block):
        return layer(block, gain_row, up_index, up_pairs, down_index, down_pairs)

    return apply


def per_device(activations, keep, gains, up_rows, up_blocks, down_rows, down_blocks):
    up_all, down_all = gather_weights(up_blocks, down_blocks)
    apply = make_layer(
        gains[0], up_rows[0].reshape(-1), up_all, down_rows[0].reshape(-1), down_all
    )
    places = jnp.cumsum(keep) - 1
    target = jnp.where(keep == 1, places, KEEP_DEV)
    chosen = (
        jnp.zeros((KEEP_DEV + 1,), jnp.int32)
        .at[target]
        .set(jnp.arange(keep.shape[0], dtype=jnp.int32))[:KEEP_DEV]
    )
    selected = activations[chosen]
    width = selected.shape[1]
    section = lax.axis_index(SEC)
    sections = lax.axis_size(SEC)
    pieces = 4
    group_rows = selected.shape[0] // pieces
    split = selected.reshape(pieces, group_rows, width)

    def advance(turn, held, record):
        offset = turn - section
        entry = jnp.where(section == 0, split[jnp.minimum(turn, pieces - 1)], held)
        active = (offset >= 0) & (offset < pieces)
        result = lax.cond(active, apply, jnp.zeros_like, entry)
        slot = jnp.clip(offset, 0, pieces - 1)
        current = lax.dynamic_index_in_dim(record, slot, 0, keepdims=False)
        updated = jnp.where(active, result, current)
        record = lax.dynamic_update_index_in_dim(record, updated, slot, 0)
        return (result, record)

    def turn_step(turn, carry):
        held, record = carry
        result, record = advance(turn, held, record)
        held = from_behind(result, SEC, 1)
        return (held, record)

    turns = sections + pieces - 1
    held, record = lax.fori_loop(0, turns, turn_step, (split[0], split))
    final = record.reshape(selected.shape[0], width)
    merged = activations.at[chosen].set(final)
    return merged[None]


def solution(mesh):
    zh = 4
    yc = mesh.shape["fsdp"] // zh
    zl = 2
    xs = mesh.shape["section"] // zl
    devices = mesh.devices.reshape(zl, xs, zh, yc // 2, 2)
    fine = Mesh(devices, ("zl", "x", "zh", "y", "c"))
    return jax.shard_map(
        per_device,
        mesh=fine,
        in_specs=(
            P(FS, None),
            P(FS),
            P(SEC, None),
            P(SEC, None, None),
            P(SEC, FS, None),
            P(SEC, None, None),
            P(SEC, FS, None),
        ),
        out_specs=P(SEC, FS, None),
        check_vma=False,
    )
```

```python
import jax
import jax.numpy as jnp
from jax import lax
from jax.experimental import pallas as pl
from jax.experimental.pallas import tpu as pltpu
from jax.sharding import Mesh
from jax.sharding import PartitionSpec as P

BLK = 64
UP_DEPTH = 2
DOWN_DEPTH = 2
KEEP_DEV = 128

SEC = ("zl", "x")
FS = ("zh", "y", "c")


def from_behind(value, axis, steps):
    count = lax.axis_size(axis)
    initial, last = (max(0, -steps), min(count, count - steps))
    return lax.ppermute(value, axis, [(source, source + steps) for source in range(initial, last)])


def exchange_zh(part):
    count = lax.axis_size("zh")
    own = lax.axis_index("zh")
    got = [part]
    for shift in range(1, count):
        got.append(lax.ppermute(part, "zh", [(i, (i + shift) % count) for i in range(count)]))
    stacked = jnp.stack(got)
    order = (own - jnp.arange(count, dtype=jnp.int32)) % count
    return jnp.take(stacked, order, axis=0)


def gather_weights(up_shard, down_shard):
    cols = up_shard.shape[1] // UP_DEPTH
    up_part = up_shard.reshape(cols, UP_DEPTH, BLK, BLK).transpose(0, 3, 1, 2)
    up_part = up_part.reshape(cols * BLK, UP_DEPTH * BLK)
    count = down_shard.shape[1]
    blocks = down_shard.reshape(count, BLK, BLK).transpose(0, 2, 1)
    zeros = jnp.zeros_like(blocks)
    first = lax.axis_index(FS) * count + jnp.arange(count, dtype=jnp.int32)
    odd = (first % DOWN_DEPTH == 1)[:, None, None]
    placed = jnp.where(odd, jnp.concatenate([zeros, blocks], axis=2), jnp.concatenate([blocks, zeros], axis=2))
    down_part = placed.reshape(count * BLK, DOWN_DEPTH * BLK)
    split = up_part.shape[0]
    full = exchange_zh(jnp.concatenate([up_part, down_part], axis=0))
    full = lax.all_gather(full[:, None], ("y", "c"), axis=1, tiled=True)
    up_full = full[:, :, :split].reshape(-1, BLK, UP_DEPTH * BLK)
    down_full = full[:, :, split:].reshape(-1, DOWN_DEPTH, BLK, DOWN_DEPTH * BLK)
    return up_full, down_full[:, 0] + down_full[:, 1]


LANE = 128
NT = (((1,), (1,)), ((), ()))


def _gelu(v):
    return 0.5 * v * (1.0 + jnp.tanh(0.7978845608028654 * (v + 0.044715 * (v * v * v))))


def _pick(s_ref, a, b, lane):
    left = s_ref[a % 2, (a + 1) // 2]
    right = s_ref[1 - b % 2, b // 2]
    return jnp.where(lane < BLK, left, right)


def _shifted(prev, cur):
    lane = lax.broadcasted_iota(jnp.int32, cur.shape, 1)
    return jnp.where(lane < BLK, pltpu.roll(prev, BLK, 1), pltpu.roll(cur, BLK, 1))


UP_CHUNKS = 4
DOWN_CHUNKS = 2


def _layer_kernel(up_idx, dn_idx, x_ref, g_ref, wu_hbm, wd_hbm, o_ref, sx_ref, sh_ref, wu_ref, wd_ref, sems):
    count, width = x_ref.shape
    pairs_in = width // LANE
    pairs_hid = wu_ref.shape[0]
    up_step = pairs_hid // UP_CHUNKS
    down_step = pairs_in // DOWN_CHUNKS
    copies = []
    for k in range(UP_CHUNKS):
        part = pl.ds(k * up_step, up_step)
        copies.append(pltpu.make_async_copy(wu_hbm.at[part], wu_ref.at[part], sems.at[k]))
    for k in range(DOWN_CHUNKS):
        part = pl.ds(k * down_step, down_step)
        copies.append(pltpu.make_async_copy(wd_hbm.at[part], wd_ref.at[part], sems.at[UP_CHUNKS + k]))
    for copy in copies:
        copy.start()
    x = x_ref[...].astype(jnp.float32)
    scale = lax.rsqrt(jnp.mean(x * x, axis=1, keepdims=True) + 1e-05)
    zero = jnp.zeros((count, LANE), jnp.bfloat16)
    prev = zero
    for p in range(pairs_in):
        cur = (x[:, p * LANE:(p + 1) * LANE] * scale * g_ref[:, p * LANE:(p + 1) * LANE]).astype(jnp.bfloat16)
        sx_ref[0, p] = cur
        sx_ref[1, p] = _shifted(prev, cur)
        prev = cur
    sx_ref[0, pairs_in] = zero
    sx_ref[1, pairs_in] = _shifted(prev, zero)
    lane = lax.broadcasted_iota(jnp.int32, (count, LANE), 1)

    def up(cp, prev):
        c0 = 2 * cp
        l0 = _pick(sx_ref, up_idx[2 * c0], up_idx[2 * c0 + 1], lane)
        l1 = _pick(sx_ref, up_idx[2 * c0 + 2], up_idx[2 * c0 + 3], lane)
        s = lax.dot_general(jnp.concatenate([l0, l1], axis=0), wu_ref[cp], NT, preferred_element_type=jnp.float32)
        cur = _gelu(jnp.where(lane < BLK, s[:count], s[count:])).astype(jnp.bfloat16)
        sh_ref[0, cp] = cur
        sh_ref[1, cp] = _shifted(prev, cur)
        return cur

    last = zero
    for k in range(UP_CHUNKS):
        copies[k].wait()
        last = lax.fori_loop(k * up_step, (k + 1) * up_step, up, last, unroll=24)
    sh_ref[0, pairs_hid] = zero
    sh_ref[1, pairs_hid] = _shifted(last, zero)

    for cp in range(pairs_in):
        if cp % down_step == 0:
            copies[UP_CHUNKS + cp // down_step].wait()
        c0 = 2 * cp
        l0 = _pick(sh_ref, dn_idx[2 * c0], dn_idx[2 * c0 + 1], lane)
        l1 = _pick(sh_ref, dn_idx[2 * c0 + 2], dn_idx[2 * c0 + 3], lane)
        s = lax.dot_general(jnp.concatenate([l0, l1], axis=0), wd_ref[cp], NT, preferred_element_type=jnp.float32)
        s = jnp.where(lane < BLK, s[:count], s[count:])
        o_ref[:, cp * LANE:(cp + 1) * LANE] = (x[:, cp * LANE:(cp + 1) * LANE] + s).astype(jnp.bfloat16)


def as_pairs(wt):
    return wt.reshape(wt.shape[0] // 2, 2 * BLK, LANE)


def layer(x, gain_row, up_idx, wu_p, dn_idx, wd_p):
    count, width = x.shape
    pairs_in = width // LANE
    pairs_hid = wu_p.shape[0]
    return pl.pallas_call(
        _layer_kernel,
        out_shape=jax.ShapeDtypeStruct((count, width), jnp.bfloat16),
        grid_spec=pltpu.PrefetchScalarGridSpec(
            num_scalar_prefetch=2,
            grid=(1,),
            in_specs=[
                pl.BlockSpec((count, width), lambda i, u, d: (0, 0)),
                pl.BlockSpec((1, width), lambda i, u, d: (0, 0)),
                pl.BlockSpec(memory_space=pl.ANY),
                pl.BlockSpec(memory_space=pl.ANY),
            ],
            out_specs=pl.BlockSpec((count, width), lambda i, u, d: (0, 0)),
            scratch_shapes=[
                pltpu.VMEM((2, pairs_in + 1, count, LANE), jnp.bfloat16),
                pltpu.VMEM((2, pairs_hid + 1, count, LANE), jnp.bfloat16),
                pltpu.VMEM(wu_p.shape, wu_p.dtype),
                pltpu.VMEM(wd_p.shape, wd_p.dtype),
                pltpu.SemaphoreType.DMA((UP_CHUNKS + DOWN_CHUNKS,)),
            ],
        ),
        compiler_params=pltpu.CompilerParams(vmem_limit_bytes=40 * 1024 * 1024),
    )(up_idx, dn_idx, x, gain_row, wu_p, wd_p)


def make_layer(gain, up_index, up_cols, down_index, down_cols):
    gain_row = gain.astype(jnp.float32)[None, :]
    up_pairs = as_pairs(up_cols)
    down_pairs = as_pairs(down_cols)

    def apply(block):
        return layer(block, gain_row, up_index, up_pairs, down_index, down_pairs)

    return apply


def per_device(activations, keep, gains, up_rows, up_blocks, down_rows, down_blocks):
    up_all, down_all = gather_weights(up_blocks, down_blocks)
    apply = make_layer(
        gains[0], up_rows[0].reshape(-1), up_all, down_rows[0].reshape(-1), down_all
    )
    places = jnp.cumsum(keep) - 1
    target = jnp.where(keep == 1, places, KEEP_DEV)
    chosen = (
        jnp.zeros((KEEP_DEV + 1,), jnp.int32)
        .at[target]
        .set(jnp.arange(keep.shape[0], dtype=jnp.int32))[:KEEP_DEV]
    )
    selected = activations[chosen]
    width = selected.shape[1]
    section = lax.axis_index(SEC)
    sections = lax.axis_size(SEC)
    pieces = 4
    group_rows = selected.shape[0] // pieces
    split = selected.reshape(pieces, group_rows, width)

    def advance(turn, held, record):
        offset = turn - section
        entry = jnp.where(section == 0, split[jnp.minimum(turn, pieces - 1)], held)
        active = (offset >= 0) & (offset < pieces)
        result = lax.cond(active, apply, jnp.zeros_like, entry)
        slot = jnp.clip(offset, 0, pieces - 1)
        current = lax.dynamic_index_in_dim(record, slot, 0, keepdims=False)
        updated = jnp.where(active, result, current)
        record = lax.dynamic_update_index_in_dim(record, updated, slot, 0)
        return (result, record)

    def turn_step(turn, carry):
        held, record = carry
        result, record = advance(turn, held, record)
        held = from_behind(result, SEC, 1)
        return (held, record)

    turns = sections + pieces - 1
    held, record = lax.fori_loop(0, turns, turn_step, (split[0], split))
    final = record.reshape(selected.shape[0], width)
    merged = activations.at[chosen].set(final)
    return merged[None]


def solution(mesh):
    zh = 4
    yc = mesh.shape["fsdp"] // zh
    zl = 2
    xs = mesh.shape["section"] // zl
    devices = mesh.devices.reshape(zl, xs, zh, yc // 2, 2)
    fine = Mesh(devices, ("zl", "x", "zh", "y", "c"))
    return jax.shard_map(
        per_device,
        mesh=fine,
        in_specs=(
            P(FS, None),
            P(FS),
            P(SEC, None),
            P(SEC, None, None),
            P(SEC, FS, None),
            P(SEC, None, None),
            P(SEC, FS, None),
        ),
        out_specs=P(SEC, FS, None),
        check_vma=False,
    )
```

```python
import jax
import jax.numpy as jnp
from jax import lax
from jax.experimental import pallas as pl
from jax.experimental.pallas import tpu as pltpu
from jax.sharding import Mesh
from jax.sharding import PartitionSpec as P

BLK = 64
UP_DEPTH = 2
DOWN_DEPTH = 2
KEEP_DEV = 128

SEC = ("zl", "x")
FS = ("zh", "y", "c")


def from_behind(value, axis, steps):
    count = lax.axis_size(axis)
    initial, last = (max(0, -steps), min(count, count - steps))
    return lax.ppermute(value, axis, [(source, source + steps) for source in range(initial, last)])


def exchange_zh(part):
    count = lax.axis_size("zh")
    own = lax.axis_index("zh")
    got = [part]
    for shift in range(1, count):
        got.append(lax.ppermute(part, "zh", [(i, (i + shift) % count) for i in range(count)]))
    stacked = jnp.stack(got)
    order = (own - jnp.arange(count, dtype=jnp.int32)) % count
    return jnp.take(stacked, order, axis=0)


def gather_weights(up_shard, down_shard):
    cols = up_shard.shape[1] // UP_DEPTH
    up_part = up_shard.reshape(cols, UP_DEPTH, BLK, BLK).transpose(0, 3, 1, 2)
    up_part = up_part.reshape(cols * BLK, UP_DEPTH * BLK)
    count = down_shard.shape[1]
    blocks = down_shard.reshape(count, BLK, BLK).transpose(0, 2, 1)
    zeros = jnp.zeros_like(blocks)
    first = lax.axis_index(FS) * count + jnp.arange(count, dtype=jnp.int32)
    odd = (first % DOWN_DEPTH == 1)[:, None, None]
    placed = jnp.where(odd, jnp.concatenate([zeros, blocks], axis=2), jnp.concatenate([blocks, zeros], axis=2))
    down_part = placed.reshape(count * BLK, DOWN_DEPTH * BLK)
    split = up_part.shape[0]
    full = exchange_zh(jnp.concatenate([up_part, down_part], axis=0))
    full = lax.all_gather(full[:, None], ("y", "c"), axis=1, tiled=True)
    up_full = full[:, :, :split].reshape(-1, BLK, UP_DEPTH * BLK)
    down_full = full[:, :, split:].reshape(-1, DOWN_DEPTH, BLK, DOWN_DEPTH * BLK)
    return up_full, down_full[:, 0] + down_full[:, 1]


LANE = 128
NT = (((1,), (1,)), ((), ()))


def _gelu(v):
    return 0.5 * v * (1.0 + jnp.tanh(0.7978845608028654 * (v + 0.044715 * (v * v * v))))


def _pick(s_ref, a, b, lane):
    left = s_ref[a % 2, (a + 1) // 2]
    right = s_ref[1 - b % 2, b // 2]
    return jnp.where(lane < BLK, left, right)


def _shifted(prev, cur):
    lane = lax.broadcasted_iota(jnp.int32, cur.shape, 1)
    return jnp.where(lane < BLK, pltpu.roll(prev, BLK, 1), pltpu.roll(cur, BLK, 1))


UP_CHUNKS = 4
DOWN_CHUNKS = 2


def _layer_kernel(up_idx, dn_idx, x_ref, g_ref, wu_hbm, wd_hbm, o_ref, sx_ref, sh_ref, wu_ref, wd_ref, sems):
    count, width = x_ref.shape
    pairs_in = width // LANE
    pairs_hid = wu_ref.shape[0]
    up_step = pairs_hid // UP_CHUNKS
    down_step = pairs_in // DOWN_CHUNKS
    copies = []
    for k in range(UP_CHUNKS):
        part = pl.ds(k * up_step, up_step)
        copies.append(pltpu.make_async_copy(wu_hbm.at[part], wu_ref.at[part], sems.at[k]))
    for k in range(DOWN_CHUNKS):
        part = pl.ds(k * down_step, down_step)
        copies.append(pltpu.make_async_copy(wd_hbm.at[part], wd_ref.at[part], sems.at[UP_CHUNKS + k]))
    for copy in copies:
        copy.start()
    x = x_ref[...].astype(jnp.float32)
    scale = lax.rsqrt(jnp.mean(x * x, axis=1, keepdims=True) + 1e-05)
    zero = jnp.zeros((count, LANE), jnp.bfloat16)
    prev = zero
    for p in range(pairs_in):
        cur = (x[:, p * LANE:(p + 1) * LANE] * scale * g_ref[:, p * LANE:(p + 1) * LANE]).astype(jnp.bfloat16)
        sx_ref[0, p] = cur
        sx_ref[1, p] = _shifted(prev, cur)
        prev = cur
    sx_ref[0, pairs_in] = zero
    sx_ref[1, pairs_in] = _shifted(prev, zero)
    lane = lax.broadcasted_iota(jnp.int32, (count, LANE), 1)

    def up(cp, prev):
        c0 = 2 * cp
        l0 = _pick(sx_ref, up_idx[2 * c0], up_idx[2 * c0 + 1], lane)
        l1 = _pick(sx_ref, up_idx[2 * c0 + 2], up_idx[2 * c0 + 3], lane)
        s = lax.dot_general(jnp.concatenate([l0, l1], axis=0), wu_ref[cp], NT, preferred_element_type=jnp.float32)
        cur = _gelu(jnp.where(lane < BLK, s[:count], s[count:])).astype(jnp.bfloat16)
        sh_ref[0, cp] = cur
        sh_ref[1, cp] = _shifted(prev, cur)
        return cur

    last = zero
    for k in range(UP_CHUNKS):
        copies[k].wait()
        last = lax.fori_loop(k * up_step, (k + 1) * up_step, up, last, unroll=24)
    sh_ref[0, pairs_hid] = zero
    sh_ref[1, pairs_hid] = _shifted(last, zero)

    for cp in range(pairs_in):
        if cp % down_step == 0:
            copies[UP_CHUNKS + cp // down_step].wait()
        c0 = 2 * cp
        l0 = _pick(sh_ref, dn_idx[2 * c0], dn_idx[2 * c0 + 1], lane)
        l1 = _pick(sh_ref, dn_idx[2 * c0 + 2], dn_idx[2 * c0 + 3], lane)
        s = lax.dot_general(jnp.concatenate([l0, l1], axis=0), wd_ref[cp], NT, preferred_element_type=jnp.float32)
        s = jnp.where(lane < BLK, s[:count], s[count:])
        o_ref[:, cp * LANE:(cp + 1) * LANE] = (x[:, cp * LANE:(cp + 1) * LANE] + s).astype(jnp.bfloat16)


def as_pairs(wt):
    return wt.reshape(wt.shape[0] // 2, 2 * BLK, LANE)


def layer(x, gain_row, up_idx, wu_p, dn_idx, wd_p):
    count, width = x.shape
    pairs_in = width // LANE
    pairs_hid = wu_p.shape[0]
    return pl.pallas_call(
        _layer_kernel,
        out_shape=jax.ShapeDtypeStruct((count, width), jnp.bfloat16),
        grid_spec=pltpu.PrefetchScalarGridSpec(
            num_scalar_prefetch=2,
            grid=(1,),
            in_specs=[
                pl.BlockSpec((count, width), lambda i, u, d: (0, 0)),
                pl.BlockSpec((1, width), lambda i, u, d: (0, 0)),
                pl.BlockSpec(memory_space=pl.ANY),
                pl.BlockSpec(memory_space=pl.ANY),
            ],
            out_specs=pl.BlockSpec((count, width), lambda i, u, d: (0, 0)),
            scratch_shapes=[
                pltpu.VMEM((2, pairs_in + 1, count, LANE), jnp.bfloat16),
                pltpu.VMEM((2, pairs_hid + 1, count, LANE), jnp.bfloat16),
                pltpu.VMEM(wu_p.shape, wu_p.dtype),
                pltpu.VMEM(wd_p.shape, wd_p.dtype),
                pltpu.SemaphoreType.DMA((UP_CHUNKS + DOWN_CHUNKS,)),
            ],
        ),
        compiler_params=pltpu.CompilerParams(vmem_limit_bytes=40 * 1024 * 1024),
    )(up_idx, dn_idx, x, gain_row, wu_p, wd_p)


def make_layer(gain, up_index, up_cols, down_index, down_cols):
    gain_row = gain.astype(jnp.float32)[None, :]
    up_pairs = as_pairs(up_cols)
    down_pairs = as_pairs(down_cols)

    def apply(block):
        return layer(block, gain_row, up_index, up_pairs, down_index, down_pairs)

    return apply


def per_device(activations, keep, gains, up_rows, up_blocks, down_rows, down_blocks):
    up_all, down_all = gather_weights(up_blocks, down_blocks)
    apply = make_layer(
        gains[0], up_rows[0].reshape(-1), up_all, down_rows[0].reshape(-1), down_all
    )
    places = jnp.cumsum(keep) - 1
    target = jnp.where(keep == 1, places, KEEP_DEV)
    chosen = (
        jnp.zeros((KEEP_DEV + 1,), jnp.int32)
        .at[target]
        .set(jnp.arange(keep.shape[0], dtype=jnp.int32))[:KEEP_DEV]
    )
    selected = activations[chosen]
    width = selected.shape[1]
    section = lax.axis_index(SEC)
    sections = lax.axis_size(SEC)
    pieces = 4
    group_rows = selected.shape[0] // pieces
    split = selected.reshape(pieces, group_rows, width)

    def advance(turn, held, record):
        offset = turn - section
        entry = jnp.where(section == 0, split[jnp.minimum(turn, pieces - 1)], held)
        active = (offset >= 0) & (offset < pieces)
        result = lax.cond(active, apply, jnp.zeros_like, entry)
        slot = jnp.clip(offset, 0, pieces - 1)
        current = lax.dynamic_index_in_dim(record, slot, 0, keepdims=False)
        updated = jnp.where(active, result, current)
        record = lax.dynamic_update_index_in_dim(record, updated, slot, 0)
        return (result, record)

    def turn_step(turn, carry):
        held, record = carry
        result, record = advance(turn, held, record)
        held = from_behind(result, SEC, 1)
        return (held, record)

    turns = sections + pieces - 1
    held, record = lax.fori_loop(0, turns, turn_step, (split[0], split))
    final = record.reshape(selected.shape[0], width)
    rows = final[jnp.clip(places, 0, KEEP_DEV - 1)]
    merged = jnp.where((keep == 1)[:, None], rows, activations)
    return merged[None]


def solution(mesh):
    zh = 4
    yc = mesh.shape["fsdp"] // zh
    zl = 2
    xs = mesh.shape["section"] // zl
    devices = mesh.devices.reshape(zl, xs, zh, yc // 2, 2)
    fine = Mesh(devices, ("zl", "x", "zh", "y", "c"))
    return jax.shard_map(
        per_device,
        mesh=fine,
        in_specs=(
            P(FS, None),
            P(FS),
            P(SEC, None),
            P(SEC, None, None),
            P(SEC, FS, None),
            P(SEC, None, None),
            P(SEC, FS, None),
        ),
        out_specs=P(SEC, FS, None),
        check_vma=False,
    )
```

```python
import jax
import jax.numpy as jnp
from jax import lax
from jax.experimental import pallas as pl
from jax.experimental.pallas import tpu as pltpu
from jax.sharding import Mesh
from jax.sharding import PartitionSpec as P

BLK = 64
UP_DEPTH = 2
DOWN_DEPTH = 2
KEEP_DEV = 128

SEC = ("zl", "x")
FS = ("zh", "y", "c")


def from_behind(value, axis, steps):
    count = lax.axis_size(axis)
    initial, last = (max(0, -steps), min(count, count - steps))
    return lax.ppermute(value, axis, [(source, source + steps) for source in range(initial, last)])


def exchange_zh(part):
    count = lax.axis_size("zh")
    own = lax.axis_index("zh")
    got = [part]
    for shift in range(1, count):
        got.append(lax.ppermute(part, "zh", [(i, (i + shift) % count) for i in range(count)]))
    stacked = jnp.stack(got)
    order = (own - jnp.arange(count, dtype=jnp.int32)) % count
    return jnp.take(stacked, order, axis=0)


def gather_weights(up_shard, down_shard):
    cols = up_shard.shape[1] // UP_DEPTH
    up_part = up_shard.reshape(cols, UP_DEPTH, BLK, BLK).transpose(0, 3, 1, 2)
    up_part = up_part.reshape(cols * BLK, UP_DEPTH * BLK)
    count = down_shard.shape[1]
    blocks = down_shard.reshape(count, BLK, BLK).transpose(0, 2, 1)
    zeros = jnp.zeros_like(blocks)
    first = lax.axis_index(FS) * count + jnp.arange(count, dtype=jnp.int32)
    odd = (first % DOWN_DEPTH == 1)[:, None, None]
    placed = jnp.where(odd, jnp.concatenate([zeros, blocks], axis=2), jnp.concatenate([blocks, zeros], axis=2))
    down_part = placed.reshape(count * BLK, DOWN_DEPTH * BLK)
    split = up_part.shape[0]
    full = exchange_zh(jnp.concatenate([up_part, down_part], axis=0))
    full = lax.all_gather(full[:, None], ("y", "c"), axis=1, tiled=True)
    up_full = full[:, :, :split].reshape(-1, BLK, UP_DEPTH * BLK)
    down_full = full[:, :, split:].reshape(-1, DOWN_DEPTH, BLK, DOWN_DEPTH * BLK)
    return up_full, down_full[:, 0] + down_full[:, 1]


LANE = 128
NT = (((1,), (1,)), ((), ()))


def _gelu(v):
    return 0.5 * v * (1.0 + jnp.tanh(0.7978845608028654 * (v + 0.044715 * (v * v * v))))


def _pick(s_ref, a, b, lane):
    left = s_ref[a % 2, (a + 1) // 2]
    right = s_ref[1 - b % 2, b // 2]
    return jnp.where(lane < BLK, left, right)


def _shifted(prev, cur):
    lane = lax.broadcasted_iota(jnp.int32, cur.shape, 1)
    return jnp.where(lane < BLK, pltpu.roll(prev, BLK, 1), pltpu.roll(cur, BLK, 1))


UP_CHUNKS = 2
DOWN_CHUNKS = 2


def _layer_kernel(up_idx, dn_idx, x_ref, g_ref, wu_hbm, wd_hbm, o_ref, sx_ref, sh_ref, wu_ref, wd_ref, sems):
    count, width = x_ref.shape
    pairs_in = width // LANE
    pairs_hid = wu_ref.shape[0]
    up_step = pairs_hid // UP_CHUNKS
    down_step = pairs_in // DOWN_CHUNKS
    copies = []
    for k in range(UP_CHUNKS):
        part = pl.ds(k * up_step, up_step)
        copies.append(pltpu.make_async_copy(wu_hbm.at[part], wu_ref.at[part], sems.at[k]))
    for k in range(DOWN_CHUNKS):
        part = pl.ds(k * down_step, down_step)
        copies.append(pltpu.make_async_copy(wd_hbm.at[part], wd_ref.at[part], sems.at[UP_CHUNKS + k]))
    for copy in copies:
        copy.start()
    x = x_ref[...].astype(jnp.float32)
    scale = lax.rsqrt(jnp.mean(x * x, axis=1, keepdims=True) + 1e-05)
    zero = jnp.zeros((count, LANE), jnp.bfloat16)
    prev = zero
    for p in range(pairs_in):
        cur = (x[:, p * LANE:(p + 1) * LANE] * scale * g_ref[:, p * LANE:(p + 1) * LANE]).astype(jnp.bfloat16)
        sx_ref[0, p] = cur
        sx_ref[1, p] = _shifted(prev, cur)
        prev = cur
    sx_ref[0, pairs_in] = zero
    sx_ref[1, pairs_in] = _shifted(prev, zero)
    lane = lax.broadcasted_iota(jnp.int32, (count, LANE), 1)

    def up(cp, prev):
        c0 = 2 * cp
        l0 = _pick(sx_ref, up_idx[2 * c0], up_idx[2 * c0 + 1], lane)
        l1 = _pick(sx_ref, up_idx[2 * c0 + 2], up_idx[2 * c0 + 3], lane)
        s = lax.dot_general(jnp.concatenate([l0, l1], axis=0), wu_ref[cp], NT, preferred_element_type=jnp.float32)
        cur = _gelu(jnp.where(lane < BLK, s[:count], s[count:])).astype(jnp.bfloat16)
        sh_ref[0, cp] = cur
        sh_ref[1, cp] = _shifted(prev, cur)
        return cur

    last = zero
    for k in range(UP_CHUNKS):
        copies[k].wait()
        last = lax.fori_loop(k * up_step, (k + 1) * up_step, up, last, unroll=48)
    sh_ref[0, pairs_hid] = zero
    sh_ref[1, pairs_hid] = _shifted(last, zero)

    for cp in range(pairs_in):
        if cp % down_step == 0:
            copies[UP_CHUNKS + cp // down_step].wait()
        c0 = 2 * cp
        l0 = _pick(sh_ref, dn_idx[2 * c0], dn_idx[2 * c0 + 1], lane)
        l1 = _pick(sh_ref, dn_idx[2 * c0 + 2], dn_idx[2 * c0 + 3], lane)
        s = lax.dot_general(jnp.concatenate([l0, l1], axis=0), wd_ref[cp], NT, preferred_element_type=jnp.float32)
        s = jnp.where(lane < BLK, s[:count], s[count:])
        o_ref[:, cp * LANE:(cp + 1) * LANE] = (x[:, cp * LANE:(cp + 1) * LANE] + s).astype(jnp.bfloat16)


def as_pairs(wt):
    return wt.reshape(wt.shape[0] // 2, 2 * BLK, LANE)


def layer(x, gain_row, up_idx, wu_p, dn_idx, wd_p):
    count, width = x.shape
    pairs_in = width // LANE
    pairs_hid = wu_p.shape[0]
    return pl.pallas_call(
        _layer_kernel,
        out_shape=jax.ShapeDtypeStruct((count, width), jnp.bfloat16),
        grid_spec=pltpu.PrefetchScalarGridSpec(
            num_scalar_prefetch=2,
            grid=(1,),
            in_specs=[
                pl.BlockSpec((count, width), lambda i, u, d: (0, 0)),
                pl.BlockSpec((1, width), lambda i, u, d: (0, 0)),
                pl.BlockSpec(memory_space=pl.ANY),
                pl.BlockSpec(memory_space=pl.ANY),
            ],
            out_specs=pl.BlockSpec((count, width), lambda i, u, d: (0, 0)),
            scratch_shapes=[
                pltpu.VMEM((2, pairs_in + 1, count, LANE), jnp.bfloat16),
                pltpu.VMEM((2, pairs_hid + 1, count, LANE), jnp.bfloat16),
                pltpu.VMEM(wu_p.shape, wu_p.dtype),
                pltpu.VMEM(wd_p.shape, wd_p.dtype),
                pltpu.SemaphoreType.DMA((UP_CHUNKS + DOWN_CHUNKS,)),
            ],
        ),
        compiler_params=pltpu.CompilerParams(vmem_limit_bytes=40 * 1024 * 1024),
    )(up_idx, dn_idx, x, gain_row, wu_p, wd_p)


def make_layer(gain, up_index, up_cols, down_index, down_cols):
    gain_row = gain.astype(jnp.float32)[None, :]
    up_pairs = as_pairs(up_cols)
    down_pairs = as_pairs(down_cols)

    def apply(block):
        return layer(block, gain_row, up_index, up_pairs, down_index, down_pairs)

    return apply


def per_device(activations, keep, gains, up_rows, up_blocks, down_rows, down_blocks):
    up_all, down_all = gather_weights(up_blocks, down_blocks)
    apply = make_layer(
        gains[0], up_rows[0].reshape(-1), up_all, down_rows[0].reshape(-1), down_all
    )
    places = jnp.cumsum(keep) - 1
    target = jnp.where(keep == 1, places, KEEP_DEV)
    chosen = (
        jnp.zeros((KEEP_DEV + 1,), jnp.int32)
        .at[target]
        .set(jnp.arange(keep.shape[0], dtype=jnp.int32))[:KEEP_DEV]
    )
    selected = activations[chosen]
    width = selected.shape[1]
    section = lax.axis_index(SEC)
    sections = lax.axis_size(SEC)
    pieces = 4
    group_rows = selected.shape[0] // pieces
    split = selected.reshape(pieces, group_rows, width)

    def advance(turn, held, record):
        offset = turn - section
        entry = jnp.where(section == 0, split[jnp.minimum(turn, pieces - 1)], held)
        active = (offset >= 0) & (offset < pieces)
        result = lax.cond(active, apply, jnp.zeros_like, entry)
        slot = jnp.clip(offset, 0, pieces - 1)
        current = lax.dynamic_index_in_dim(record, slot, 0, keepdims=False)
        updated = jnp.where(active, result, current)
        record = lax.dynamic_update_index_in_dim(record, updated, slot, 0)
        return (result, record)

    def turn_step(turn, carry):
        held, record = carry
        result, record = advance(turn, held, record)
        held = from_behind(result, SEC, 1)
        return (held, record)

    turns = sections + pieces - 1
    held, record = lax.fori_loop(0, turns, turn_step, (split[0], split))
    final = record.reshape(selected.shape[0], width)
    merged = activations.at[chosen].set(final)
    return merged[None]


def solution(mesh):
    zh = 4
    yc = mesh.shape["fsdp"] // zh
    zl = 2
    xs = mesh.shape["section"] // zl
    devices = mesh.devices.reshape(zl, xs, zh, yc // 2, 2)
    fine = Mesh(devices, ("zl", "x", "zh", "y", "c"))
    return jax.shard_map(
        per_device,
        mesh=fine,
        in_specs=(
            P(FS, None),
            P(FS),
            P(SEC, None),
            P(SEC, None, None),
            P(SEC, FS, None),
            P(SEC, None, None),
            P(SEC, FS, None),
        ),
        out_specs=P(SEC, FS, None),
        check_vma=False,
    )
```
